128 devices in a mesh: dp: 16 (over x, y), feat: 8 (over z, core).
Axes of the slice: x: 4, y: 4, z: 4, core: 2. Of those that a mesh axis runs over, the one named last changes fastest.
Arguments:
- images: bfloat16 [8192, 3072], P(('dp', 'feat')), may hold values from -6 to 6
- labels: int32 [8192], P('dp'), may hold values from 0 to 999
- predictions: float32 [8192, 1000], P('dp'), may hold values from -2 to 2
- filters: bfloat16 [75, 1024], P(None, 'feat'), may hold values from -0.75 to 0.75
- biases: float32 [1024], P('feat'), may hold values from -3 to 3
Outputs:
- weights: float32 [4096, 1000], P('feat')
- new_residual: float32 [8192, 1000], P(('dp', 'feat'))
The draws below stay inside these ranges and needn't reach their ends.
All inputs are finite; a program needn't handle non-finite values.
Results may differ from the reference program's by a relative error of at most 0.007.
The reference program's roundings to bfloat16 on the way count: a program that leaves them out, or rounds other values in their place, can miss the bound.
Values may be sent and summed in bfloat16 or wider, within the bound.
No kernel may reach another device: no remote copies, remote signals or barrier semaphores. Data moves between devices by JAX's collectives and lax.ppermute only.
A program may use at most 192 MiB of HBM per device.

```python
import jax
import jax.numpy as jnp
from jax import lax

SIDE = 32
CHAN = 3
KSIZE = 5
FILT = 128
CLASSES = 1000
FEATB = 512
IMAGES = 8192
BLOCKS = 8


def touch_ends(values, key, least, high):
    extent = values.shape
    place = [jax.random.randint(jax.random.fold_in(key, axis), (), 0, extent[axis]) for axis in range(len(extent))]
    values = values.at[tuple(place)].set(least)
    longest = extent.index(max(extent))
    place[longest] = (place[longest] + 1) % extent[longest]
    return values.at[tuple(place)].set(high)


def level_of(own_key, dims, pieces, low, high):
    level = 1.0
    for axis_at, blocks in pieces:
        draws = jax.random.uniform(jax.random.fold_in(jax.random.fold_in(own_key, 6), axis_at), (blocks,), jnp.float32, low / len(pieces), high / len(pieces))
        level = level * jnp.repeat(jnp.exp(draws), dims[axis_at] // blocks).reshape((-1,) + (1,) * (len(dims) - 1 - axis_at))
    return level


def noise(rng, extent, width, bound, cuts=(), kind=jnp.bfloat16):
    drawn = width * jax.random.normal(rng, extent, jnp.float32)
    if cuts:
        drawn = drawn * level_of(rng, extent, cuts, -0.22, 0.18)
    return jnp.clip(drawn, -bound, bound).astype(kind)


def setup_inputs(seed: int = 0) -> dict:
    key_of = jax.random.split(jax.random.key(seed), 6)
    images = noise(key_of[0], (IMAGES, SIDE * SIDE * CHAN), 1.0, 6.0, ((0, 128),))
    labels = touch_ends(jax.random.randint(key_of[1], (IMAGES,), 0, CLASSES), jax.random.fold_in(key_of[1], 1), 0, CLASSES - 1).astype(jnp.int32)
    predictions = noise(key_of[2], (IMAGES, CLASSES), 0.3, 2.0, ((0, 16),), jnp.float32)
    filters = noise(key_of[3], (KSIZE * KSIZE * CHAN, BLOCKS * FILT), (KSIZE * KSIZE * CHAN) ** -0.5, 0.75, ((1, 8),))
    biases = noise(key_of[4], (BLOCKS * FILT,), 0.5, 3.0, ((0, 8),), jnp.float32)
    return dict(images=images, labels=labels, predictions=predictions, filters=filters, biases=biases)


def chol_solve(factor, rhs):
    middle = lax.linalg.triangular_solve(factor, rhs, left_side=True, lower=True, transpose_a=False)
    return lax.linalg.triangular_solve(factor, middle, left_side=True, lower=True, transpose_a=True)

def split_parts(values):
    upper = values.astype(jnp.bfloat16)
    lower = (values - upper.astype(jnp.float32)).astype(jnp.bfloat16)
    return (upper, lower)

def left_product(feats, other):
    return lax.dot_general(feats.astype(jnp.float32), other.astype(jnp.float32), (((0,), (0,)), ((), ())), preferred_element_type=jnp.float32)

def conv_pool(imgs, kernel, offsets):
    count = imgs.shape[0]
    pics = imgs.reshape(count, SIDE, SIDE, CHAN)
    response = lax.conv_general_dilated(pics, kernel, (1, 1), 'VALID', dimension_numbers=('NHWC', 'HWIO', 'NHWC'), preferred_element_type=jnp.float32)
    response = jnp.maximum(response + offsets, 0.0)
    half = (SIDE - KSIZE + 1) // 2
    pooled = response.reshape(count, 2, half, 2, half, FILT).mean(axis=(2, 4))
    return jnp.transpose(pooled, (0, 3, 1, 2)).reshape(count, 4 * FILT).astype(jnp.bfloat16)

def reference(images, labels, predictions, filters, biases):
    residual = (labels[:, None] == jnp.arange(CLASSES, dtype=jnp.int32)[None, :]).astype(jnp.float32) - predictions
    res_upper, res_lower = split_parts(residual)
    group = 16

    def one_block(index):
        kernel = lax.dynamic_slice_in_dim(filters, index * FILT, FILT, 1).reshape(KSIZE, KSIZE, CHAN, FILT)
        offsets = lax.dynamic_slice_in_dim(biases, index * FILT, FILT, 0)
        blocks = images.reshape(IMAGES // group, group, SIDE * SIDE * CHAN)
        feats = lax.map(lambda part: conv_pool(part, kernel, offsets), blocks).reshape(IMAGES, FEATB)
        gram = left_product(feats, feats)
        gram = gram / IMAGES + 0.5 * jnp.eye(FEATB, dtype=jnp.float32)
        cross = (left_product(feats, res_upper) + left_product(feats, res_lower)) / IMAGES
        factor = jnp.linalg.cholesky(gram)
        solved = chol_solve(factor, cross)
        sol_upper, sol_lower = split_parts(solved)
        fit = jnp.dot(feats.astype(jnp.float32), sol_upper.astype(jnp.float32), preferred_element_type=jnp.float32) + jnp.dot(feats.astype(jnp.float32), sol_lower.astype(jnp.float32), preferred_element_type=jnp.float32)
        return (solved, fit)

    def step(total, index):
        solved, fit = one_block(index)
        return (total + fit, solved)
    total, solved_all = lax.scan(step, jnp.zeros((IMAGES, CLASSES), jnp.float32), jnp.arange(BLOCKS, dtype=jnp.int32))
    return (solved_all.reshape(BLOCKS * FEATB, CLASSES), residual - total)
```

```python
import math

import jax
import jax.numpy as jnp
from jax import lax
from jax.sharding import PartitionSpec as P

SIDE = 32
CHAN = 3
KSIZE = 5


def chol_solve(factor, rhs):
    middle = lax.linalg.triangular_solve(factor, rhs, left_side=True, lower=True, transpose_a=False)
    return lax.linalg.triangular_solve(factor, middle, left_side=True, lower=True, transpose_a=True)


def split_parts(values):
    upper = values.astype(jnp.bfloat16)
    lower = (values - upper.astype(jnp.float32)).astype(jnp.bfloat16)
    return (upper, lower)


def left_product(feats, other):
    return lax.dot_general(
        feats, other, (((0,), (0,)), ((), ())), preferred_element_type=jnp.float32
    )


def conv_pool(imgs, kernel, offsets):
    count = imgs.shape[0]
    filt_count = kernel.shape[3]
    pics = imgs.reshape(count, SIDE, SIDE, CHAN)
    response = lax.conv_general_dilated(
        pics,
        kernel,
        (1, 1),
        "VALID",
        dimension_numbers=("NHWC", "HWIO", "NHWC"),
        preferred_element_type=jnp.float32,
    )
    response = jnp.maximum(response + offsets, 0.0)
    half = (SIDE - KSIZE + 1) // 2
    pooled = response.reshape(count, 2, half, 2, half, filt_count).mean(axis=(2, 4))
    return jnp.transpose(pooled, (0, 3, 1, 2)).reshape(count, 4 * filt_count).astype(jnp.bfloat16)


def shards(images, labels, predictions, filters, biases):
    filt_count = filters.shape[1]
    kernel = filters.reshape(KSIZE, KSIZE, CHAN, filt_count)
    share = images.shape[0]
    total_images = share * lax.axis_size("feat") * lax.axis_size("dp")
    piece = lax.all_gather(images, "feat", axis=0, tiled=True)
    count = piece.shape[0]
    group = math.gcd(count, 128)
    blocks = piece.reshape(count // group, group, piece.shape[1])
    out = lax.map(lambda part: conv_pool(part, kernel, biases), blocks)
    feats = out.reshape(count, 4 * filt_count)
    width = feats.shape[1]
    residual = (
        labels[:, None] == jnp.arange(predictions.shape[1], dtype=jnp.int32)[None, :]
    ).astype(jnp.float32) - predictions
    res_upper, res_lower = split_parts(residual)
    gram = lax.psum(left_product(feats, feats), "dp")
    cross = left_product(feats, res_upper) + left_product(feats, res_lower)
    cross, gram = lax.optimization_barrier((cross, gram))
    cross = lax.psum(cross, "dp")
    gram = gram / total_images + 0.5 * jnp.eye(width, dtype=jnp.float32)
    cross = cross / total_images
    factor = jnp.linalg.cholesky(gram)
    solved = chol_solve(factor, cross)
    sol_upper, sol_lower = split_parts(solved)
    fitted = lax.psum_scatter(
        (
            jnp.dot(feats, sol_upper, preferred_element_type=jnp.float32)
            + jnp.dot(feats, sol_lower, preferred_element_type=jnp.float32)
        ).astype(jnp.bfloat16),
        "feat",
        scatter_dimension=0,
        tiled=True,
    ).astype(jnp.float32)
    mine = lax.dynamic_slice_in_dim(residual, lax.axis_index("feat") * share, share, 0)
    return (solved, mine - fitted)


def solution(mesh):
    placed = (P(("dp", "feat"), None), P("dp"), P("dp", None), P(None, "feat"), P("feat"))
    return jax.shard_map(
        shards,
        mesh=mesh,
        in_specs=placed,
        out_specs=(P("feat", None), P(("dp", "feat"), None)),
        check_vma=False,
    )
```

```python
import functools
import math

import jax
import jax.numpy as jnp
from jax import lax
from jax.experimental import pallas as pl
from jax.experimental.pallas import tpu as pltpu
from jax.sharding import PartitionSpec as P

SIDE = 32
CHAN = 3
KSIZE = 5


OUT = SIDE - KSIZE + 1
CHUNK = 7
SPAN = (CHUNK + KSIZE - 1) * CHAN
PITCH = 48
DEPTH = KSIZE * PITCH
TILE = 256


def band_weights(filters, offsets):
    filt_count = filters.shape[1]
    taps = filters.reshape(KSIZE, KSIZE * CHAN, filt_count)
    hi = lax.reduce_precision(offsets, exponent_bits=8, mantissa_bits=7)
    mid = lax.reduce_precision(offsets - hi, exponent_bits=8, mantissa_bits=7)
    lo = offsets - hi - mid
    bias_rows = jnp.stack([hi, mid, lo]).astype(filters.dtype)
    gap = PITCH - SPAN - 3
    blocks = []
    for col in range(CHUNK):
        lead = jnp.zeros((col * CHAN, filt_count), filters.dtype)
        fill = jnp.zeros((SPAN - col * CHAN - KSIZE * CHAN, filt_count), filters.dtype)
        rest = jnp.zeros((PITCH - SPAN, filt_count), filters.dtype)
        first = [lead, taps[0], fill, bias_rows, jnp.zeros((gap, filt_count), filters.dtype)]
        later = [part for ky in range(1, KSIZE) for part in (lead, taps[ky], fill, rest)]
        blocks.append(jnp.concatenate(first + later, axis=0))
    return jnp.transpose(jnp.stack(blocks, axis=0), (0, 2, 1)).reshape(CHUNK * filt_count, DEPTH)


def image_strips(imgs):
    count = imgs.shape[0]
    pics = imgs.reshape(count, SIDE, SIDE * CHAN)
    ones = jnp.ones((count, SIDE, 3), imgs.dtype)
    zeros = jnp.zeros((count, SIDE, PITCH - SPAN - 3), imgs.dtype)
    strips = [
        jnp.concatenate([pics[:, :, CHUNK * CHAN * j: CHUNK * CHAN * j + SPAN], ones, zeros], axis=2)
        for j in range(OUT // CHUNK)
    ]
    stacked = jnp.stack(strips, axis=0)
    return jnp.transpose(stacked, (0, 2, 3, 1)).reshape(OUT // CHUNK, SIDE * PITCH, count)


def pool_kernel(strip_ref, band_ref, out_ref, acc_ref):
    filt_count = out_ref.shape[1]
    half = OUT // 2
    acc_ref[...] = jnp.zeros_like(acc_ref)
    band = band_ref[...]

    def row_step(r, carry, top):
        start = pl.multiple_of(r * PITCH, 16)
        for j in range(OUT // CHUNK):
            patch = strip_ref[j, pl.ds(start, DEPTH), :]
            resp = jnp.dot(band, patch, preferred_element_type=jnp.float32)
            resp = jnp.maximum(resp, 0.0)
            part = resp[0:filt_count]
            for col in range(1, CHUNK):
                part = part + resp[col * filt_count:(col + 1) * filt_count]
            quad = top * 2 + (1 if j >= (OUT // CHUNK) // 2 else 0)
            acc_ref[quad] += part
        return carry

    lax.fori_loop(0, half, functools.partial(row_step, top=0), 0)
    lax.fori_loop(half, OUT, functools.partial(row_step, top=1), 0)
    out_ref[...] = (acc_ref[...] * (1.0 / float(half * half))).astype(out_ref.dtype)


def conv_pool_fused(imgs, filters, offsets):
    count = imgs.shape[0]
    filt_count = filters.shape[1]
    strips = image_strips(imgs)
    band = band_weights(filters, offsets)
    pooled = pl.pallas_call(
        pool_kernel,
        grid=(count // TILE,),
        in_specs=[
            pl.BlockSpec((OUT // CHUNK, SIDE * PITCH, TILE), lambda i: (0, 0, i)),
            pl.BlockSpec((CHUNK * filt_count, DEPTH), lambda i: (0, 0)),
        ],
        out_specs=pl.BlockSpec((4, filt_count, TILE), lambda i: (0, 0, i)),
        out_shape=jax.ShapeDtypeStruct((4, filt_count, count), jnp.bfloat16),
        scratch_shapes=[pltpu.VMEM((4, filt_count, TILE), jnp.float32)],
    )(strips, band)
    return jnp.transpose(pooled, (2, 1, 0)).reshape(count, 4 * filt_count)


def chol_solve(factor, rhs):
    middle = lax.linalg.triangular_solve(factor, rhs, left_side=True, lower=True, transpose_a=False)
    return lax.linalg.triangular_solve(factor, middle, left_side=True, lower=True, transpose_a=True)


def split_parts(values):
    upper = values.astype(jnp.bfloat16)
    lower = (values - upper.astype(jnp.float32)).astype(jnp.bfloat16)
    return (upper, lower)


def left_product(feats, other):
    return lax.dot_general(
        feats, other, (((0,), (0,)), ((), ())), preferred_element_type=jnp.float32
    )


def shards(images, labels, predictions, filters, biases):
    share = images.shape[0]
    total_images = share * lax.axis_size("feat") * lax.axis_size("dp")
    piece = lax.all_gather(images, "feat", axis=0, tiled=True)
    feats = conv_pool_fused(piece, filters, biases)
    width = feats.shape[1]
    residual = (
        labels[:, None] == jnp.arange(predictions.shape[1], dtype=jnp.int32)[None, :]
    ).astype(jnp.float32) - predictions
    res_upper, res_lower = split_parts(residual)
    gram = left_product(feats, feats)
    cross = left_product(feats, res_upper) + left_product(feats, res_lower)
    gram, cross = lax.psum((gram, cross), "dp")
    gram = gram / total_images + 0.5 * jnp.eye(width, dtype=jnp.float32)
    cross = cross / total_images
    factor = jnp.linalg.cholesky(gram)
    solved = chol_solve(factor, cross)
    sol_upper, sol_lower = split_parts(solved)
    fitted = lax.psum_scatter(
        (
            jnp.dot(feats, sol_upper, preferred_element_type=jnp.float32)
            + jnp.dot(feats, sol_lower, preferred_element_type=jnp.float32)
        ).astype(jnp.bfloat16),
        "feat",
        scatter_dimension=0,
        tiled=True,
    ).astype(jnp.float32)
    mine = lax.dynamic_slice_in_dim(residual, lax.axis_index("feat") * share, share, 0)
    return (solved, mine - fitted)


def solution(mesh):
    placed = (P(("dp", "feat"), None), P("dp"), P("dp", None), P(None, "feat"), P("feat"))
    return jax.shard_map(
        shards,
        mesh=mesh,
        in_specs=placed,
        out_specs=(P("feat", None), P(("dp", "feat"), None)),
        check_vma=False,
    )
```

```python
import functools
import math

import jax
import jax.numpy as jnp
from jax import lax
from jax.experimental import pallas as pl
from jax.experimental.pallas import tpu as pltpu
from jax.sharding import PartitionSpec as P

SIDE = 32
CHAN = 3
KSIZE = 5


OUT = SIDE - KSIZE + 1
CHUNK = 7
SPAN = (CHUNK + KSIZE - 1) * CHAN
PITCH = 48
DEPTH = KSIZE * PITCH
TILE = 256


def band_weights(filters, offsets):
    filt_count = filters.shape[1]
    taps = filters.reshape(KSIZE, KSIZE * CHAN, filt_count)
    hi = lax.reduce_precision(offsets, exponent_bits=8, mantissa_bits=7)
    mid = lax.reduce_precision(offsets - hi, exponent_bits=8, mantissa_bits=7)
    lo = offsets - hi - mid
    bias_rows = jnp.stack([hi, mid, lo]).astype(filters.dtype)
    gap = PITCH - SPAN - 3
    blocks = []
    for col in range(CHUNK):
        lead = jnp.zeros((col * CHAN, filt_count), filters.dtype)
        fill = jnp.zeros((SPAN - col * CHAN - KSIZE * CHAN, filt_count), filters.dtype)
        rest = jnp.zeros((PITCH - SPAN, filt_count), filters.dtype)
        first = [lead, taps[0], fill, bias_rows, jnp.zeros((gap, filt_count), filters.dtype)]
        later = [part for ky in range(1, KSIZE) for part in (lead, taps[ky], fill, rest)]
        blocks.append(jnp.concatenate(first + later, axis=0))
    return jnp.transpose(jnp.stack(blocks, axis=0), (0, 2, 1)).reshape(CHUNK * filt_count, DEPTH)


def image_strips(imgs):
    count = imgs.shape[0]
    pics = imgs.reshape(count, SIDE, SIDE * CHAN)
    ones = jnp.ones((count, SIDE, 3), imgs.dtype)
    zeros = jnp.zeros((count, SIDE, PITCH - SPAN - 3), imgs.dtype)
    strips = [
        jnp.concatenate([pics[:, :, CHUNK * CHAN * j: CHUNK * CHAN * j + SPAN], ones, zeros], axis=2)
        for j in range(OUT // CHUNK)
    ]
    stacked = jnp.stack(strips, axis=0)
    return jnp.transpose(stacked, (0, 2, 3, 1)).reshape(OUT // CHUNK, SIDE * PITCH, count)


def pool_kernel(strip_ref, band_ref, out_ref, acc_ref):
    filt_count = out_ref.shape[1]
    half = OUT // 2
    acc_ref[...] = jnp.zeros_like(acc_ref)
    band = band_ref[...]

    def row_step(r, carry, top):
        start = pl.multiple_of(r * PITCH, 16)
        for j in range(OUT // CHUNK):
            patch = strip_ref[j, pl.ds(start, DEPTH), :]
            resp = jnp.dot(band, patch, preferred_element_type=jnp.float32)
            resp = jnp.maximum(resp, 0.0)
            part = resp[0:filt_count]
            for col in range(1, CHUNK):
                part = part + resp[col * filt_count:(col + 1) * filt_count]
            quad = top * 2 + (1 if j >= (OUT // CHUNK) // 2 else 0)
            acc_ref[quad] += part
        return carry

    lax.fori_loop(0, half, functools.partial(row_step, top=0), 0)
    lax.fori_loop(half, OUT, functools.partial(row_step, top=1), 0)
    out_ref[...] = (acc_ref[...] * (1.0 / float(half * half))).astype(out_ref.dtype)


def conv_pool_fused(imgs, filters, offsets):
    count = imgs.shape[0]
    filt_count = filters.shape[1]
    strips = image_strips(imgs)
    band = band_weights(filters, offsets)
    pooled = pl.pallas_call(
        pool_kernel,
        grid=(count // TILE,),
        in_specs=[
            pl.BlockSpec((OUT // CHUNK, SIDE * PITCH, TILE), lambda i: (0, 0, i)),
            pl.BlockSpec((CHUNK * filt_count, DEPTH), lambda i: (0, 0)),
        ],
        out_specs=pl.BlockSpec((4, filt_count, TILE), lambda i: (0, 0, i)),
        out_shape=jax.ShapeDtypeStruct((4, filt_count, count), jnp.bfloat16),
        scratch_shapes=[pltpu.VMEM((4, filt_count, TILE), jnp.float32)],
    )(strips, band)
    return jnp.transpose(pooled, (2, 1, 0)).reshape(count, 4 * filt_count)


def chol_solve(factor, rhs):
    middle = lax.linalg.triangular_solve(factor, rhs, left_side=True, lower=True, transpose_a=False)
    return lax.linalg.triangular_solve(factor, middle, left_side=True, lower=True, transpose_a=True)


def split_parts(values):
    upper = values.astype(jnp.bfloat16)
    lower = (values - upper.astype(jnp.float32)).astype(jnp.bfloat16)
    return (upper, lower)


def left_product(feats, other):
    return lax.dot_general(
        feats, other, (((0,), (0,)), ((), ())), preferred_element_type=jnp.float32
    )


def shards(images, labels, predictions, filters, biases):
    share = images.shape[0]
    total_images = share * lax.axis_size("feat") * lax.axis_size("dp")
    piece = lax.all_gather(images, "feat", axis=0, tiled=True)
    feats = conv_pool_fused(piece, filters, biases)
    width = feats.shape[1]
    residual = (
        labels[:, None] == jnp.arange(predictions.shape[1], dtype=jnp.int32)[None, :]
    ).astype(jnp.float32) - predictions
    res_upper, res_lower = split_parts(residual)
    gram = left_product(feats, feats)
    cross = left_product(feats, res_upper) + left_product(feats, res_lower)
    both = jnp.concatenate([gram, cross], axis=1)
    both = lax.psum_scatter(both, "dp", scatter_dimension=0, tiled=True)
    both = lax.all_gather(both, "dp", axis=0, tiled=True)
    gram, cross = both[:, :width], both[:, width:]
    gram = gram / total_images + 0.5 * jnp.eye(width, dtype=jnp.float32)
    cross = cross / total_images
    factor = jnp.linalg.cholesky(gram)
    solved = chol_solve(factor, cross)
    sol_upper, sol_lower = split_parts(solved)
    fitted = lax.psum_scatter(
        (
            jnp.dot(feats, sol_upper, preferred_element_type=jnp.float32)
            + jnp.dot(feats, sol_lower, preferred_element_type=jnp.float32)
        ).astype(jnp.bfloat16),
        "feat",
        scatter_dimension=0,
        tiled=True,
    ).astype(jnp.float32)
    mine = lax.dynamic_slice_in_dim(residual, lax.axis_index("feat") * share, share, 0)
    return (solved, mine - fitted)


def solution(mesh):
    placed = (P(("dp", "feat"), None), P("dp"), P("dp", None), P(None, "feat"), P("feat"))
    return jax.shard_map(
        shards,
        mesh=mesh,
        in_specs=placed,
        out_specs=(P("feat", None), P(("dp", "feat"), None)),
        check_vma=False,
    )
```

```python
import functools
import math

import jax
import jax.numpy as jnp
from jax import lax
from jax.experimental import pallas as pl
from jax.experimental.pallas import tpu as pltpu
from jax.sharding import PartitionSpec as P

SIDE = 32
CHAN = 3
KSIZE = 5


OUT = SIDE - KSIZE + 1
CHUNK = 7
SPAN = (CHUNK + KSIZE - 1) * CHAN
PITCH = 48
DEPTH = KSIZE * PITCH
TILE = 256


def band_weights(filters, offsets):
    filt_count = filters.shape[1]
    taps = filters.reshape(KSIZE, KSIZE * CHAN, filt_count)
    hi = lax.reduce_precision(offsets, exponent_bits=8, mantissa_bits=7)
    mid = lax.reduce_precision(offsets - hi, exponent_bits=8, mantissa_bits=7)
    lo = offsets - hi - mid
    bias_rows = jnp.stack([hi, mid, lo]).astype(filters.dtype)
    gap = PITCH - SPAN - 3
    blocks = []
    for col in range(CHUNK):
        lead = jnp.zeros((col * CHAN, filt_count), filters.dtype)
        fill = jnp.zeros((SPAN - col * CHAN - KSIZE * CHAN, filt_count), filters.dtype)
        rest = jnp.zeros((PITCH - SPAN, filt_count), filters.dtype)
        first = [lead, taps[0], fill, bias_rows, jnp.zeros((gap, filt_count), filters.dtype)]
        later = [part for ky in range(1, KSIZE) for part in (lead, taps[ky], fill, rest)]
        blocks.append(jnp.concatenate(first + later, axis=0))
    return jnp.transpose(jnp.stack(blocks, axis=0), (0, 2, 1)).reshape(CHUNK * filt_count, DEPTH)


def image_strips(imgs):
    count = imgs.shape[0]
    pics = imgs.reshape(count, SIDE, SIDE * CHAN)
    ones = jnp.ones((count, SIDE, 3), imgs.dtype)
    zeros = jnp.zeros((count, SIDE, PITCH - SPAN - 3), imgs.dtype)
    strips = [
        jnp.concatenate([pics[:, :, CHUNK * CHAN * j: CHUNK * CHAN * j + SPAN], ones, zeros], axis=2)
        for j in range(OUT // CHUNK)
    ]
    stacked = jnp.stack(strips, axis=0)
    return jnp.transpose(stacked, (0, 2, 3, 1)).reshape(OUT // CHUNK, SIDE * PITCH, count)


def pool_kernel(strip_ref, band_ref, out_ref, acc_ref):
    filt_count = out_ref.shape[1]
    half = OUT // 2
    acc_ref[...] = jnp.zeros_like(acc_ref)
    band = band_ref[...]

    def row_step(r, carry, top):
        start = pl.multiple_of(r * PITCH, 16)
        for j in range(OUT // CHUNK):
            patch = strip_ref[j, pl.ds(start, DEPTH), :]
            resp = jnp.dot(band, patch, preferred_element_type=jnp.float32)
            resp = jnp.maximum(resp, 0.0)
            part = resp[0:filt_count]
            for col in range(1, CHUNK):
                part = part + resp[col * filt_count:(col + 1) * filt_count]
            quad = top * 2 + (1 if j >= (OUT // CHUNK) // 2 else 0)
            acc_ref[quad] += part
        return carry

    lax.fori_loop(0, half, functools.partial(row_step, top=0), 0)
    lax.fori_loop(half, OUT, functools.partial(row_step, top=1), 0)
    out_ref[...] = (acc_ref[...] * (1.0 / float(half * half))).astype(out_ref.dtype)


def conv_pool_fused(imgs, filters, offsets):
    count = imgs.shape[0]
    filt_count = filters.shape[1]
    strips = image_strips(imgs)
    band = band_weights(filters, offsets)
    pooled = pl.pallas_call(
        pool_kernel,
        grid=(count // TILE,),
        in_specs=[
            pl.BlockSpec((OUT // CHUNK, SIDE * PITCH, TILE), lambda i: (0, 0, i)),
            pl.BlockSpec((CHUNK * filt_count, DEPTH), lambda i: (0, 0)),
        ],
        out_specs=pl.BlockSpec((4, filt_count, TILE), lambda i: (0, 0, i)),
        out_shape=jax.ShapeDtypeStruct((4, filt_count, count), jnp.bfloat16),
        scratch_shapes=[pltpu.VMEM((4, filt_count, TILE), jnp.float32)],
    )(strips, band)
    return jnp.transpose(pooled, (2, 1, 0)).reshape(count, 4 * filt_count)


BLOCK = 128


def exact_dot(left, right):
    return jnp.dot(left, right, precision=lax.Precision.HIGHEST, preferred_element_type=jnp.float32)


def chol_solve_blocked(gram, rhs):
    size = gram.shape[0]
    count = size // BLOCK
    work = (gram + gram.T) * 0.5
    lower = {}
    inverse = []
    eye = jnp.eye(BLOCK, dtype=jnp.float32)
    for k in range(count):
        lo, hi = k * BLOCK, (k + 1) * BLOCK
        diag = jnp.linalg.cholesky(work[lo:hi, lo:hi], symmetrize_input=False)
        inv = lax.linalg.triangular_solve(diag, eye, left_side=True, lower=True, transpose_a=False)
        lower[k, k] = diag
        inverse.append(inv)
        if hi < size:
            panel = exact_dot(work[hi:, lo:hi], inv.T)
            for i in range(k + 1, count):
                lower[i, k] = panel[(i - k - 1) * BLOCK:(i - k) * BLOCK]
            work = work.at[hi:, hi:].add(-exact_dot(panel, panel.T))
    middle = []
    for k in range(count):
        part = rhs[k * BLOCK:(k + 1) * BLOCK]
        for j in range(k):
            part = part - exact_dot(lower[k, j], middle[j])
        middle.append(exact_dot(inverse[k], part))
    solved = [None] * count
    for k in reversed(range(count)):
        part = middle[k]
        for j in range(k + 1, count):
            part = part - exact_dot(lower[j, k].T, solved[j])
        solved[k] = exact_dot(inverse[k].T, part)
    return jnp.concatenate(solved, axis=0)


def split_parts(values):
    upper = values.astype(jnp.bfloat16)
    lower = (values - upper.astype(jnp.float32)).astype(jnp.bfloat16)
    return (upper, lower)


def left_product(feats, other):
    return lax.dot_general(
        feats, other, (((0,), (0,)), ((), ())), preferred_element_type=jnp.float32
    )


def shards(images, labels, predictions, filters, biases):
    share = images.shape[0]
    total_images = share * lax.axis_size("feat") * lax.axis_size("dp")
    piece = lax.all_gather(images, "feat", axis=0, tiled=True)
    feats = conv_pool_fused(piece, filters, biases)
    width = feats.shape[1]
    residual = (
        labels[:, None] == jnp.arange(predictions.shape[1], dtype=jnp.int32)[None, :]
    ).astype(jnp.float32) - predictions
    res_upper, res_lower = split_parts(residual)
    gram = left_product(feats, feats)
    cross = left_product(feats, res_upper) + left_product(feats, res_lower)
    gram, cross = lax.psum((gram, cross), "dp")
    gram = gram / total_images + 0.5 * jnp.eye(width, dtype=jnp.float32)
    cross = cross / total_images
    solved = chol_solve_blocked(gram, cross)
    sol_upper, sol_lower = split_parts(solved)
    fitted = lax.psum_scatter(
        (
            jnp.dot(feats, sol_upper, preferred_element_type=jnp.float32)
            + jnp.dot(feats, sol_lower, preferred_element_type=jnp.float32)
        ).astype(jnp.bfloat16),
        "feat",
        scatter_dimension=0,
        tiled=True,
    ).astype(jnp.float32)
    mine = lax.dynamic_slice_in_dim(residual, lax.axis_index("feat") * share, share, 0)
    return (solved, mine - fitted)


def solution(mesh):
    placed = (P(("dp", "feat"), None), P("dp"), P("dp", None), P(None, "feat"), P("feat"))
    return jax.shard_map(
        shards,
        mesh=mesh,
        in_specs=placed,
        out_specs=(P("feat", None), P(("dp", "feat"), None)),
        check_vma=False,
    )
```

```python
import functools
import math

import jax
import jax.numpy as jnp
from jax import lax
from jax.experimental import pallas as pl
from jax.experimental.pallas import tpu as pltpu
from jax.sharding import PartitionSpec as P

SIDE = 32
CHAN = 3
KSIZE = 5


OUT = SIDE - KSIZE + 1
CHUNK = 7
SPAN = (CHUNK + KSIZE - 1) * CHAN
PITCH = 48
DEPTH = KSIZE * PITCH
TILE = 256


def band_weights(filters, offsets):
    filt_count = filters.shape[1]
    taps = filters.reshape(KSIZE, KSIZE * CHAN, filt_count)
    hi = lax.reduce_precision(offsets, exponent_bits=8, mantissa_bits=7)
    mid = lax.reduce_precision(offsets - hi, exponent_bits=8, mantissa_bits=7)
    lo = offsets - hi - mid
    bias_rows = jnp.stack([hi, mid, lo]).astype(filters.dtype)
    gap = PITCH - SPAN - 3
    blocks = []
    for col in range(CHUNK):
        lead = jnp.zeros((col * CHAN, filt_count), filters.dtype)
        fill = jnp.zeros((SPAN - col * CHAN - KSIZE * CHAN, filt_count), filters.dtype)
        rest = jnp.zeros((PITCH - SPAN, filt_count), filters.dtype)
        first = [lead, taps[0], fill, bias_rows, jnp.zeros((gap, filt_count), filters.dtype)]
        later = [part for ky in range(1, KSIZE) for part in (lead, taps[ky], fill, rest)]
        blocks.append(jnp.concatenate(first + later, axis=0))
    return jnp.transpose(jnp.stack(blocks, axis=0), (0, 2, 1)).reshape(CHUNK * filt_count, DEPTH)


def image_strips(imgs):
    count = imgs.shape[0]
    pics = imgs.reshape(count, SIDE, SIDE * CHAN)
    ones = jnp.ones((count, SIDE, 3), imgs.dtype)
    zeros = jnp.zeros((count, SIDE, PITCH - SPAN - 3), imgs.dtype)
    strips = [
        jnp.concatenate([pics[:, :, CHUNK * CHAN * j: CHUNK * CHAN * j + SPAN], ones, zeros], axis=2)
        for j in range(OUT // CHUNK)
    ]
    stacked = jnp.stack(strips, axis=0)
    return jnp.transpose(stacked, (0, 2, 3, 1)).reshape(OUT // CHUNK, SIDE * PITCH, count)


def pool_kernel(strip_ref, band_ref, out_ref, acc_ref):
    filt_count = out_ref.shape[1]
    half = OUT // 2
    acc_ref[...] = jnp.zeros_like(acc_ref)
    band = band_ref[...]

    def row_step(r, carry, top):
        start = pl.multiple_of(r * PITCH, 16)
        for j in range(OUT // CHUNK):
            patch = strip_ref[j, pl.ds(start, DEPTH), :]
            resp = jnp.dot(band, patch, preferred_element_type=jnp.float32)
            resp = jnp.maximum(resp, 0.0)
            part = resp[0:filt_count]
            for col in range(1, CHUNK):
                part = part + resp[col * filt_count:(col + 1) * filt_count]
            quad = top * 2 + (1 if j >= (OUT // CHUNK) // 2 else 0)
            acc_ref[quad] += part
        return carry

    lax.fori_loop(0, half, functools.partial(row_step, top=0), 0)
    lax.fori_loop(half, OUT, functools.partial(row_step, top=1), 0)
    out_ref[...] = (acc_ref[...] * (1.0 / float(half * half))).astype(out_ref.dtype)


def conv_pool_fused(imgs, filters, offsets):
    count = imgs.shape[0]
    filt_count = filters.shape[1]
    strips = image_strips(imgs)
    band = band_weights(filters, offsets)
    pooled = pl.pallas_call(
        pool_kernel,
        grid=(count // TILE,),
        in_specs=[
            pl.BlockSpec((OUT // CHUNK, SIDE * PITCH, TILE), lambda i: (0, 0, i)),
            pl.BlockSpec((CHUNK * filt_count, DEPTH), lambda i: (0, 0)),
        ],
        out_specs=pl.BlockSpec((4, filt_count, TILE), lambda i: (0, 0, i)),
        out_shape=jax.ShapeDtypeStruct((4, filt_count, count), jnp.bfloat16),
        scratch_shapes=[pltpu.VMEM((4, filt_count, TILE), jnp.float32)],
    )(strips, band)
    return jnp.transpose(pooled, (2, 1, 0)).reshape(count, 4 * filt_count)


BLOCK = 64


def exact_dot(left, right):
    return jnp.dot(left, right, precision=lax.Precision.HIGHEST, preferred_element_type=jnp.float32)


def chol_solve_blocked(gram, rhs):
    size = gram.shape[0]
    count = size // BLOCK
    work = (gram + gram.T) * 0.5
    lower = {}
    inverse = []
    eye = jnp.eye(BLOCK, dtype=jnp.float32)
    for k in range(count):
        lo, hi = k * BLOCK, (k + 1) * BLOCK
        diag = jnp.linalg.cholesky(work[lo:hi, lo:hi], symmetrize_input=False)
        inv = lax.linalg.triangular_solve(diag, eye, left_side=True, lower=True, transpose_a=False)
        lower[k, k] = diag
        inverse.append(inv)
        if hi < size:
            panel = exact_dot(work[hi:, lo:hi], inv.T)
            for i in range(k + 1, count):
                lower[i, k] = panel[(i - k - 1) * BLOCK:(i - k) * BLOCK]
            work = work.at[hi:, hi:].add(-exact_dot(panel, panel.T))
    middle = []
    for k in range(count):
        part = rhs[k * BLOCK:(k + 1) * BLOCK]
        for j in range(k):
            part = part - exact_dot(lower[k, j], middle[j])
        middle.append(exact_dot(inverse[k], part))
    solved = [None] * count
    for k in reversed(range(count)):
        part = middle[k]
        for j in range(k + 1, count):
            part = part - exact_dot(lower[j, k].T, solved[j])
        solved[k] = exact_dot(inverse[k].T, part)
    return jnp.concatenate(solved, axis=0)


def split_parts(values):
    upper = values.astype(jnp.bfloat16)
    lower = (values - upper.astype(jnp.float32)).astype(jnp.bfloat16)
    return (upper, lower)


def left_product(feats, other):
    return lax.dot_general(
        feats, other, (((0,), (0,)), ((), ())), preferred_element_type=jnp.float32
    )


def shards(images, labels, predictions, filters, biases):
    share = images.shape[0]
    total_images = share * lax.axis_size("feat") * lax.axis_size("dp")
    piece = lax.all_gather(images, "feat", axis=0, tiled=True)
    feats = conv_pool_fused(piece, filters, biases)
    width = feats.shape[1]
    residual = (
        labels[:, None] == jnp.arange(predictions.shape[1], dtype=jnp.int32)[None, :]
    ).astype(jnp.float32) - predictions
    res_upper, res_lower = split_parts(residual)
    gram = left_product(feats, feats)
    cross = left_product(feats, res_upper) + left_product(feats, res_lower)
    gram, cross = lax.psum((gram, cross), "dp")
    gram = gram / total_images + 0.5 * jnp.eye(width, dtype=jnp.float32)
    cross = cross / total_images
    solved = chol_solve_blocked(gram, cross)
    sol_upper, sol_lower = split_parts(solved)
    fitted = lax.psum_scatter(
        (
            jnp.dot(feats, sol_upper, preferred_element_type=jnp.float32)
            + jnp.dot(feats, sol_lower, preferred_element_type=jnp.float32)
        ).astype(jnp.bfloat16),
        "feat",
        scatter_dimension=0,
        tiled=True,
    ).astype(jnp.float32)
    mine = lax.dynamic_slice_in_dim(residual, lax.axis_index("feat") * share, share, 0)
    return (solved, mine - fitted)


def solution(mesh):
    placed = (P(("dp", "feat"), None), P("dp"), P("dp", None), P(None, "feat"), P("feat"))
    return jax.shard_map(
        shards,
        mesh=mesh,
        in_specs=placed,
        out_specs=(P("feat", None), P(("dp", "feat"), None)),
        check_vma=False,
    )
```

```python
import functools
import math

import jax
import jax.numpy as jnp
from jax import lax
from jax.experimental import pallas as pl
from jax.experimental.pallas import tpu as pltpu
from jax.sharding import PartitionSpec as P

SIDE = 32
CHAN = 3
KSIZE = 5


OUT = SIDE - KSIZE + 1
CHUNK = 7
SPAN = (CHUNK + KSIZE - 1) * CHAN
PITCH = 48
DEPTH = KSIZE * PITCH
TILE = 256


def band_weights(filters, offsets):
    filt_count = filters.shape[1]
    taps = filters.reshape(KSIZE, KSIZE * CHAN, filt_count)
    hi = lax.reduce_precision(offsets, exponent_bits=8, mantissa_bits=7)
    mid = lax.reduce_precision(offsets - hi, exponent_bits=8, mantissa_bits=7)
    lo = offsets - hi - mid
    bias_rows = jnp.stack([hi, mid, lo]).astype(filters.dtype)
    gap = PITCH - SPAN - 3
    blocks = []
    for col in range(CHUNK):
        lead = jnp.zeros((col * CHAN, filt_count), filters.dtype)
        fill = jnp.zeros((SPAN - col * CHAN - KSIZE * CHAN, filt_count), filters.dtype)
        rest = jnp.zeros((PITCH - SPAN, filt_count), filters.dtype)
        first = [lead, taps[0], fill, bias_rows, jnp.zeros((gap, filt_count), filters.dtype)]
        later = [part for ky in range(1, KSIZE) for part in (lead, taps[ky], fill, rest)]
        blocks.append(jnp.concatenate(first + later, axis=0))
    return jnp.transpose(jnp.stack(blocks, axis=0), (0, 2, 1)).reshape(CHUNK * filt_count, DEPTH)


def image_strips(imgs):
    count = imgs.shape[0]
    rows = jnp.transpose(imgs).reshape(SIDE, SIDE * CHAN, count)
    ones = jnp.ones((SIDE, 3, count), imgs.dtype)
    zeros = jnp.zeros((SIDE, PITCH - SPAN - 3, count), imgs.dtype)
    strips = [
        jnp.concatenate([rows[:, CHUNK * CHAN * j: CHUNK * CHAN * j + SPAN], ones, zeros], axis=1)
        for j in range(OUT // CHUNK)
    ]
    return jnp.stack(strips, axis=0).reshape(OUT // CHUNK, SIDE * PITCH, count)


def pool_kernel(strip_ref, band_ref, out_ref, acc_ref):
    filt_count = out_ref.shape[1]
    half = OUT // 2
    acc_ref[...] = jnp.zeros_like(acc_ref)
    band = band_ref[...]

    def row_step(r, carry, top):
        start = pl.multiple_of(r * PITCH, 16)
        for j in range(OUT // CHUNK):
            patch = strip_ref[j, pl.ds(start, DEPTH), :]
            resp = jnp.dot(band, patch, preferred_element_type=jnp.float32)
            resp = jnp.maximum(resp, 0.0)
            part = resp[0:filt_count]
            for col in range(1, CHUNK):
                part = part + resp[col * filt_count:(col + 1) * filt_count]
            quad = top * 2 + (1 if j >= (OUT // CHUNK) // 2 else 0)
            acc_ref[quad] += part
        return carry

    lax.fori_loop(0, half, functools.partial(row_step, top=0), 0)
    lax.fori_loop(half, OUT, functools.partial(row_step, top=1), 0)
    out_ref[...] = (acc_ref[...] * (1.0 / float(half * half))).astype(out_ref.dtype)


def conv_pool_fused(imgs, filters, offsets):
    count = imgs.shape[0]
    filt_count = filters.shape[1]
    strips = image_strips(imgs)
    band = band_weights(filters, offsets)
    pooled = pl.pallas_call(
        pool_kernel,
        grid=(count // TILE,),
        in_specs=[
            pl.BlockSpec((OUT // CHUNK, SIDE * PITCH, TILE), lambda i: (0, 0, i)),
            pl.BlockSpec((CHUNK * filt_count, DEPTH), lambda i: (0, 0)),
        ],
        out_specs=pl.BlockSpec((4, filt_count, TILE), lambda i: (0, 0, i)),
        out_shape=jax.ShapeDtypeStruct((4, filt_count, count), jnp.bfloat16),
        scratch_shapes=[pltpu.VMEM((4, filt_count, TILE), jnp.float32)],
    )(strips, band)
    return jnp.transpose(pooled, (2, 1, 0)).reshape(count, 4 * filt_count)


BLOCK = 128


def exact_dot(left, right):
    return jnp.dot(left, right, precision=lax.Precision.HIGHEST, preferred_element_type=jnp.float32)


def chol_solve_blocked(gram, rhs):
    size = gram.shape[0]
    count = size // BLOCK
    work = (gram + gram.T) * 0.5
    lower = {}
    inverse = []
    eye = jnp.eye(BLOCK, dtype=jnp.float32)
    for k in range(count):
        lo, hi = k * BLOCK, (k + 1) * BLOCK
        diag = jnp.linalg.cholesky(work[lo:hi, lo:hi], symmetrize_input=False)
        inv = lax.linalg.triangular_solve(diag, eye, left_side=True, lower=True, transpose_a=False)
        lower[k, k] = diag
        inverse.append(inv)
        if hi < size:
            panel = exact_dot(work[hi:, lo:hi], inv.T)
            for i in range(k + 1, count):
                lower[i, k] = panel[(i - k - 1) * BLOCK:(i - k) * BLOCK]
            work = work.at[hi:, hi:].add(-exact_dot(panel, panel.T))
    middle = []
    for k in range(count):
        part = rhs[k * BLOCK:(k + 1) * BLOCK]
        for j in range(k):
            part = part - exact_dot(lower[k, j], middle[j])
        middle.append(exact_dot(inverse[k], part))
    solved = [None] * count
    for k in reversed(range(count)):
        part = middle[k]
        for j in range(k + 1, count):
            part = part - exact_dot(lower[j, k].T, solved[j])
        solved[k] = exact_dot(inverse[k].T, part)
    return jnp.concatenate(solved, axis=0)


def split_parts(values):
    upper = values.astype(jnp.bfloat16)
    lower = (values - upper.astype(jnp.float32)).astype(jnp.bfloat16)
    return (upper, lower)


def left_product(feats, other):
    return lax.dot_general(
        feats, other, (((0,), (0,)), ((), ())), preferred_element_type=jnp.float32
    )


def shards(images, labels, predictions, filters, biases):
    share = images.shape[0]
    total_images = share * lax.axis_size("feat") * lax.axis_size("dp")
    piece = lax.all_gather(images, "feat", axis=0, tiled=True)
    feats = conv_pool_fused(piece, filters, biases)
    width = feats.shape[1]
    residual = (
        labels[:, None] == jnp.arange(predictions.shape[1], dtype=jnp.int32)[None, :]
    ).astype(jnp.float32) - predictions
    res_upper, res_lower = split_parts(residual)
    gram = left_product(feats, feats)
    cross = left_product(feats, res_upper) + left_product(feats, res_lower)
    gram, cross = lax.psum((gram, cross), "dp")
    gram = gram / total_images + 0.5 * jnp.eye(width, dtype=jnp.float32)
    cross = cross / total_images
    solved = chol_solve_blocked(gram, cross)
    sol_upper, sol_lower = split_parts(solved)
    fitted = lax.psum_scatter(
        (
            jnp.dot(feats, sol_upper, preferred_element_type=jnp.float32)
            + jnp.dot(feats, sol_lower, preferred_element_type=jnp.float32)
        ).astype(jnp.bfloat16),
        "feat",
        scatter_dimension=0,
        tiled=True,
    ).astype(jnp.float32)
    mine = lax.dynamic_slice_in_dim(residual, lax.axis_index("feat") * share, share, 0)
    return (solved, mine - fitted)


def solution(mesh):
    placed = (P(("dp", "feat"), None), P("dp"), P("dp", None), P(None, "feat"), P("feat"))
    return jax.shard_map(
        shards,
        mesh=mesh,
        in_specs=placed,
        out_specs=(P("feat", None), P(("dp", "feat"), None)),
        check_vma=False,
    )
```

```python
import functools
import math

import jax
import jax.numpy as jnp
from jax import lax
from jax.experimental import pallas as pl
from jax.experimental.pallas import tpu as pltpu
from jax.sharding import PartitionSpec as P

SIDE = 32
CHAN = 3
KSIZE = 5


OUT = SIDE - KSIZE + 1
CHUNK = 7
SPAN = (CHUNK + KSIZE - 1) * CHAN
PITCH = 48
DEPTH = KSIZE * PITCH
TILE = 256


def band_weights(filters, offsets):
    filt_count = filters.shape[1]
    taps = filters.reshape(KSIZE, KSIZE * CHAN, filt_count)
    hi = lax.reduce_precision(offsets, exponent_bits=8, mantissa_bits=7)
    mid = lax.reduce_precision(offsets - hi, exponent_bits=8, mantissa_bits=7)
    lo = offsets - hi - mid
    bias_rows = jnp.stack([hi, mid, lo]).astype(filters.dtype)
    gap = PITCH - SPAN - 3
    blocks = []
    for col in range(CHUNK):
        lead = jnp.zeros((col * CHAN, filt_count), filters.dtype)
        fill = jnp.zeros((SPAN - col * CHAN - KSIZE * CHAN, filt_count), filters.dtype)
        rest = jnp.zeros((PITCH - SPAN, filt_count), filters.dtype)
        first = [lead, taps[0], fill, bias_rows, jnp.zeros((gap, filt_count), filters.dtype)]
        later = [part for ky in range(1, KSIZE) for part in (lead, taps[ky], fill, rest)]
        blocks.append(jnp.concatenate(first + later, axis=0))
    return jnp.transpose(jnp.stack(blocks, axis=0), (0, 2, 1)).reshape(CHUNK * filt_count, DEPTH)


def image_strips(imgs):
    count = imgs.shape[0]
    pics = imgs.reshape(count, SIDE, SIDE * CHAN)
    ones = jnp.ones((count, SIDE, 3), imgs.dtype)
    zeros = jnp.zeros((count, SIDE, PITCH - SPAN - 3), imgs.dtype)
    strips = [
        jnp.concatenate([pics[:, :, CHUNK * CHAN * j: CHUNK * CHAN * j + SPAN], ones, zeros], axis=2)
        for j in range(OUT // CHUNK)
    ]
    stacked = jnp.stack(strips, axis=0)
    return jnp.transpose(stacked, (0, 2, 3, 1)).reshape(OUT // CHUNK, SIDE * PITCH, count)


def pool_kernel(strip_ref, band_ref, out_ref, acc_ref):
    filt_count = out_ref.shape[1]
    half = OUT // 2
    acc_ref[...] = jnp.zeros_like(acc_ref)
    band = band_ref[...]

    def row_step(r, carry, top):
        start = pl.multiple_of(r * PITCH, 16)
        for j in range(OUT // CHUNK):
            patch = strip_ref[j, pl.ds(start, DEPTH), :]
            resp = jnp.dot(band, patch, preferred_element_type=jnp.float32)
            resp = jnp.maximum(resp, 0.0)
            part = resp[0:filt_count]
            for col in range(1, CHUNK):
                part = part + resp[col * filt_count:(col + 1) * filt_count]
            quad = top * 2 + (1 if j >= (OUT // CHUNK) // 2 else 0)
            acc_ref[quad] += part
        return carry

    lax.fori_loop(0, half, functools.partial(row_step, top=0), 0)
    lax.fori_loop(half, OUT, functools.partial(row_step, top=1), 0)
    out_ref[...] = (acc_ref[...] * (1.0 / float(half * half))).astype(out_ref.dtype)


def conv_pool_fused(imgs, filters, offsets):
    count = imgs.shape[0]
    filt_count = filters.shape[1]
    strips = image_strips(imgs)
    band = band_weights(filters, offsets)
    pooled = pl.pallas_call(
        pool_kernel,
        grid=(count // TILE,),
        in_specs=[
            pl.BlockSpec((OUT // CHUNK, SIDE * PITCH, TILE), lambda i: (0, 0, i)),
            pl.BlockSpec((CHUNK * filt_count, DEPTH), lambda i: (0, 0)),
        ],
        out_specs=pl.BlockSpec((4, filt_count, TILE), lambda i: (0, 0, i)),
        out_shape=jax.ShapeDtypeStruct((4, filt_count, count), jnp.bfloat16),
        scratch_shapes=[pltpu.VMEM((4, filt_count, TILE), jnp.float32)],
    )(strips, band)
    return jnp.transpose(pooled, (2, 1, 0)).reshape(count, 4 * filt_count)


BLOCK = 128


def exact_dot(left, right):
    return jnp.dot(left, right, precision=lax.Precision.HIGHEST, preferred_element_type=jnp.float32)


def chol_solve_blocked(gram, rhs):
    size = gram.shape[0]
    count = size // BLOCK
    work = (gram + gram.T) * 0.5
    lower = {}
    inverse = []
    eye = jnp.eye(BLOCK, dtype=jnp.float32)
    for k in range(count):
        lo, hi = k * BLOCK, (k + 1) * BLOCK
        diag = jnp.linalg.cholesky(work[lo:hi, lo:hi], symmetrize_input=False)
        inv = lax.linalg.triangular_solve(diag, eye, left_side=True, lower=True, transpose_a=False)
        lower[k, k] = diag
        inverse.append(inv)
        if hi < size:
            panel = exact_dot(work[hi:, lo:hi], inv.T)
            for i in range(k + 1, count):
                lower[i, k] = panel[(i - k - 1) * BLOCK:(i - k) * BLOCK]
            work = work.at[hi:, hi:].add(-exact_dot(panel, panel.T))
    middle = []
    for k in range(count):
        part = rhs[k * BLOCK:(k + 1) * BLOCK]
        for j in range(k):
            part = part - exact_dot(lower[k, j], middle[j])
        middle.append(exact_dot(inverse[k], part))
    solved = [None] * count
    for k in reversed(range(count)):
        part = middle[k]
        for j in range(k + 1, count):
            part = part - exact_dot(lower[j, k].T, solved[j])
        solved[k] = exact_dot(inverse[k].T, part)
    return jnp.concatenate(solved, axis=0)


def split_parts(values):
    upper = values.astype(jnp.bfloat16)
    lower = (values - upper.astype(jnp.float32)).astype(jnp.bfloat16)
    return (upper, lower)


def left_product(feats, other):
    return lax.dot_general(
        feats, other, (((0,), (0,)), ((), ())), preferred_element_type=jnp.float32
    )


def shards(images, labels, predictions, filters, biases):
    share = images.shape[0]
    total_images = share * lax.axis_size("feat") * lax.axis_size("dp")
    piece = lax.all_gather(images, "feat", axis=0, tiled=True)
    feats = conv_pool_fused(piece, filters, biases)
    width = feats.shape[1]
    residual = (
        labels[:, None] == jnp.arange(predictions.shape[1], dtype=jnp.int32)[None, :]
    ).astype(jnp.float32) - predictions
    res_upper, res_lower = split_parts(residual)
    gram = left_product(feats, feats)
    doubled = jnp.concatenate([feats, feats], axis=0)
    cross = left_product(doubled, jnp.concatenate([res_upper, res_lower], axis=0))
    gram, cross = lax.psum((gram, cross), "dp")
    gram = gram / total_images + 0.5 * jnp.eye(width, dtype=jnp.float32)
    cross = cross / total_images
    solved = chol_solve_blocked(gram, cross)
    sol_upper, sol_lower = split_parts(solved)
    fitted = lax.psum_scatter(
        (
            jnp.dot(
                jnp.concatenate([feats, feats], axis=1),
                jnp.concatenate([sol_upper, sol_lower], axis=0),
                preferred_element_type=jnp.float32,
            )
        ).astype(jnp.bfloat16),
        "feat",
        scatter_dimension=0,
        tiled=True,
    ).astype(jnp.float32)
    mine = lax.dynamic_slice_in_dim(residual, lax.axis_index("feat") * share, share, 0)
    return (solved, mine - fitted)


def solution(mesh):
    placed = (P(("dp", "feat"), None), P("dp"), P("dp", None), P(None, "feat"), P("feat"))
    return jax.shard_map(
        shards,
        mesh=mesh,
        in_specs=placed,
        out_specs=(P("feat", None), P(("dp", "feat"), None)),
        check_vma=False,
    )
```

```python
import functools
import math

import jax
import jax.numpy as jnp
from jax import lax
from jax.experimental import pallas as pl
from jax.experimental.pallas import tpu as pltpu
from jax.sharding import PartitionSpec as P

SIDE = 32
CHAN = 3
KSIZE = 5


OUT = SIDE - KSIZE + 1
CHUNK = 7
SPAN = (CHUNK + KSIZE - 1) * CHAN
PITCH = 48
DEPTH = KSIZE * PITCH
TILE = 256


def band_weights(filters, offsets):
    filt_count = filters.shape[1]
    taps = filters.reshape(KSIZE, KSIZE * CHAN, filt_count)
    hi = lax.reduce_precision(offsets, exponent_bits=8, mantissa_bits=7)
    mid = lax.reduce_precision(offsets - hi, exponent_bits=8, mantissa_bits=7)
    lo = offsets - hi - mid
    bias_rows = jnp.stack([hi, mid, lo]).astype(filters.dtype)
    gap = PITCH - SPAN - 3
    blocks = []
    for col in range(CHUNK):
        lead = jnp.zeros((col * CHAN, filt_count), filters.dtype)
        fill = jnp.zeros((SPAN - col * CHAN - KSIZE * CHAN, filt_count), filters.dtype)
        rest = jnp.zeros((PITCH - SPAN, filt_count), filters.dtype)
        first = [lead, taps[0], fill, bias_rows, jnp.zeros((gap, filt_count), filters.dtype)]
        later = [part for ky in range(1, KSIZE) for part in (lead, taps[ky], fill, rest)]
        blocks.append(jnp.concatenate(first + later, axis=0))
    return jnp.transpose(jnp.stack(blocks, axis=0), (0, 2, 1)).reshape(CHUNK * filt_count, DEPTH)


def image_strips(imgs):
    count = imgs.shape[0]
    pics = imgs.reshape(count, SIDE, SIDE * CHAN)
    ones = jnp.ones((count, SIDE, 3), imgs.dtype)
    zeros = jnp.zeros((count, SIDE, PITCH - SPAN - 3), imgs.dtype)
    strips = [
        jnp.concatenate([pics[:, :, CHUNK * CHAN * j: CHUNK * CHAN * j + SPAN], ones, zeros], axis=2)
        for j in range(OUT // CHUNK)
    ]
    stacked = jnp.stack(strips, axis=0)
    return jnp.transpose(stacked, (0, 2, 3, 1)).reshape(OUT // CHUNK, SIDE * PITCH, count)


def pool_kernel(strip_ref, band_ref, out_ref, acc_ref):
    filt_count = out_ref.shape[1]
    half = OUT // 2
    acc_ref[...] = jnp.zeros_like(acc_ref)
    band = band_ref[...]

    def row_step(r, carry, top):
        start = pl.multiple_of(r * PITCH, 16)
        for j in range(OUT // CHUNK):
            patch = strip_ref[j, pl.ds(start, DEPTH), :]
            resp = jnp.dot(band, patch, preferred_element_type=jnp.float32)
            resp = jnp.maximum(resp, 0.0)
            part = resp[0:filt_count]
            for col in range(1, CHUNK):
                part = part + resp[col * filt_count:(col + 1) * filt_count]
            quad = top * 2 + (1 if j >= (OUT // CHUNK) // 2 else 0)
            acc_ref[quad] += part
        return carry

    lax.fori_loop(0, half, functools.partial(row_step, top=0), 0)
    lax.fori_loop(half, OUT, functools.partial(row_step, top=1), 0)
    out_ref[...] = (acc_ref[...] * (1.0 / float(half * half))).astype(out_ref.dtype)


def conv_pool_fused(imgs, filters, offsets):
    count = imgs.shape[0]
    filt_count = filters.shape[1]
    strips = image_strips(imgs)
    band = band_weights(filters, offsets)
    pooled = pl.pallas_call(
        pool_kernel,
        grid=(count // TILE,),
        in_specs=[
            pl.BlockSpec((OUT // CHUNK, SIDE * PITCH, TILE), lambda i: (0, 0, i)),
            pl.BlockSpec((CHUNK * filt_count, DEPTH), lambda i: (0, 0)),
        ],
        out_specs=pl.BlockSpec((4, filt_count, TILE), lambda i: (0, 0, i)),
        out_shape=jax.ShapeDtypeStruct((4, filt_count, count), jnp.bfloat16),
        scratch_shapes=[pltpu.VMEM((4, filt_count, TILE), jnp.float32)],
    )(strips, band)
    return jnp.transpose(pooled, (2, 1, 0)).reshape(count, 4 * filt_count)


BLOCK = 128


def exact_dot(left, right):
    return jnp.dot(left, right, precision=lax.Precision.HIGHEST, preferred_element_type=jnp.float32)


def chol_solve_blocked(gram, rhs):
    size = gram.shape[0]
    count = size // BLOCK
    work = (gram + gram.T) * 0.5
    lower = {}
    inverse = []
    eye = jnp.eye(BLOCK, dtype=jnp.float32)
    for k in range(count):
        lo, hi = k * BLOCK, (k + 1) * BLOCK
        diag = jnp.linalg.cholesky(work[lo:hi, lo:hi], symmetrize_input=False)
        inv = lax.linalg.triangular_solve(diag, eye, left_side=True, lower=True, transpose_a=False)
        lower[k, k] = diag
        inverse.append(inv)
        if hi < size:
            panel = exact_dot(work[hi:, lo:hi], inv.T)
            for i in range(k + 1, count):
                lower[i, k] = panel[(i - k - 1) * BLOCK:(i - k) * BLOCK]
            work = work.at[hi:, hi:].add(-exact_dot(panel, panel.T))
    middle = []
    for k in range(count):
        part = rhs[k * BLOCK:(k + 1) * BLOCK]
        if k:
            left = jnp.concatenate([lower[k, j] for j in range(k)], axis=1)
            part = part - exact_dot(left, jnp.concatenate(middle, axis=0))
        middle.append(exact_dot(inverse[k], part))
    solved = [None] * count
    for k in reversed(range(count)):
        part = middle[k]
        if k + 1 < count:
            below = jnp.concatenate([lower[j, k] for j in range(k + 1, count)], axis=0)
            part = part - exact_dot(below.T, jnp.concatenate(solved[k + 1:], axis=0))
        solved[k] = exact_dot(inverse[k].T, part)
    return jnp.concatenate(solved, axis=0)


def split_parts(values):
    upper = values.astype(jnp.bfloat16)
    lower = (values - upper.astype(jnp.float32)).astype(jnp.bfloat16)
    return (upper, lower)


def left_product(feats, other):
    return lax.dot_general(
        feats, other, (((0,), (0,)), ((), ())), preferred_element_type=jnp.float32
    )


def shards(images, labels, predictions, filters, biases):
    share = images.shape[0]
    total_images = share * lax.axis_size("feat") * lax.axis_size("dp")
    piece = lax.all_gather(images, "feat", axis=0, tiled=True)
    feats = conv_pool_fused(piece, filters, biases)
    width = feats.shape[1]
    residual = (
        labels[:, None] == jnp.arange(predictions.shape[1], dtype=jnp.int32)[None, :]
    ).astype(jnp.float32) - predictions
    res_upper, res_lower = split_parts(residual)
    gram = left_product(feats, feats)
    doubled = jnp.concatenate([feats, feats], axis=0)
    cross = left_product(doubled, jnp.concatenate([res_upper, res_lower], axis=0))
    gram, cross = lax.psum((gram, cross), "dp")
    gram = gram / total_images + 0.5 * jnp.eye(width, dtype=jnp.float32)
    cross = cross / total_images
    solved = chol_solve_blocked(gram, cross)
    sol_upper, sol_lower = split_parts(solved)
    fitted = lax.psum_scatter(
        (
            jnp.dot(
                jnp.concatenate([feats, feats], axis=1),
                jnp.concatenate([sol_upper, sol_lower], axis=0),
                preferred_element_type=jnp.float32,
            )
        ).astype(jnp.bfloat16),
        "feat",
        scatter_dimension=0,
        tiled=True,
    ).astype(jnp.float32)
    mine = lax.dynamic_slice_in_dim(residual, lax.axis_index("feat") * share, share, 0)
    return (solved, mine - fitted)


def solution(mesh):
    placed = (P(("dp", "feat"), None), P("dp"), P("dp", None), P(None, "feat"), P("feat"))
    return jax.shard_map(
        shards,
        mesh=mesh,
        in_specs=placed,
        out_specs=(P("feat", None), P(("dp", "feat"), None)),
        check_vma=False,
    )
```

```python
import functools
import math

import jax
import jax.numpy as jnp
from jax import lax
from jax.experimental import pallas as pl
from jax.experimental.pallas import tpu as pltpu
from jax.sharding import PartitionSpec as P

SIDE = 32
CHAN = 3
KSIZE = 5


OUT = SIDE - KSIZE + 1
CHUNK = 7
SPAN = (CHUNK + KSIZE - 1) * CHAN
PITCH = 48
DEPTH = KSIZE * PITCH
TILE = 512


def band_weights(filters, offsets):
    filt_count = filters.shape[1]
    taps = filters.reshape(KSIZE, KSIZE * CHAN, filt_count)
    hi = lax.reduce_precision(offsets, exponent_bits=8, mantissa_bits=7)
    mid = lax.reduce_precision(offsets - hi, exponent_bits=8, mantissa_bits=7)
    lo = offsets - hi - mid
    bias_rows = jnp.stack([hi, mid, lo]).astype(filters.dtype)
    gap = PITCH - SPAN - 3
    blocks = []
    for col in range(CHUNK):
        lead = jnp.zeros((col * CHAN, filt_count), filters.dtype)
        fill = jnp.zeros((SPAN - col * CHAN - KSIZE * CHAN, filt_count), filters.dtype)
        rest = jnp.zeros((PITCH - SPAN, filt_count), filters.dtype)
        first = [lead, taps[0], fill, bias_rows, jnp.zeros((gap, filt_count), filters.dtype)]
        later = [part for ky in range(1, KSIZE) for part in (lead, taps[ky], fill, rest)]
        blocks.append(jnp.concatenate(first + later, axis=0))
    return jnp.transpose(jnp.stack(blocks, axis=0), (0, 2, 1)).reshape(CHUNK * filt_count, DEPTH)


def image_strips(imgs):
    count = imgs.shape[0]
    pics = imgs.reshape(count, SIDE, SIDE * CHAN)
    ones = jnp.ones((count, SIDE, 3), imgs.dtype)
    zeros = jnp.zeros((count, SIDE, PITCH - SPAN - 3), imgs.dtype)
    strips = [
        jnp.concatenate([pics[:, :, CHUNK * CHAN * j: CHUNK * CHAN * j + SPAN], ones, zeros], axis=2)
        for j in range(OUT // CHUNK)
    ]
    stacked = jnp.stack(strips, axis=0)
    return jnp.transpose(stacked, (0, 2, 3, 1)).reshape(OUT // CHUNK, SIDE * PITCH, count)


def pool_kernel(strip_ref, band_ref, out_ref, acc_ref):
    filt_count = out_ref.shape[1]
    half = OUT // 2
    acc_ref[...] = jnp.zeros_like(acc_ref)
    band = band_ref[...]

    def row_step(r, carry, top):
        start = pl.multiple_of(r * PITCH, 16)
        for j in range(OUT // CHUNK):
            patch = strip_ref[j, pl.ds(start, DEPTH), :]
            resp = jnp.dot(band, patch, preferred_element_type=jnp.float32)
            resp = jnp.maximum(resp, 0.0)
            part = resp[0:filt_count]
            for col in range(1, CHUNK):
                part = part + resp[col * filt_count:(col + 1) * filt_count]
            quad = top * 2 + (1 if j >= (OUT // CHUNK) // 2 else 0)
            acc_ref[quad] += part
        return carry

    lax.fori_loop(0, half, functools.partial(row_step, top=0), 0)
    lax.fori_loop(half, OUT, functools.partial(row_step, top=1), 0)
    out_ref[...] = (acc_ref[...] * (1.0 / float(half * half))).astype(out_ref.dtype)


def conv_pool_fused(imgs, filters, offsets):
    count = imgs.shape[0]
    filt_count = filters.shape[1]
    strips = image_strips(imgs)
    band = band_weights(filters, offsets)
    pooled = pl.pallas_call(
        pool_kernel,
        grid=(count // TILE,),
        in_specs=[
            pl.BlockSpec((OUT // CHUNK, SIDE * PITCH, TILE), lambda i: (0, 0, i)),
            pl.BlockSpec((CHUNK * filt_count, DEPTH), lambda i: (0, 0)),
        ],
        out_specs=pl.BlockSpec((4, filt_count, TILE), lambda i: (0, 0, i)),
        out_shape=jax.ShapeDtypeStruct((4, filt_count, count), jnp.bfloat16),
        scratch_shapes=[pltpu.VMEM((4, filt_count, TILE), jnp.float32)],
    )(strips, band)
    return jnp.transpose(pooled, (2, 1, 0)).reshape(count, 4 * filt_count)


BLOCK = 128


def exact_dot(left, right):
    return jnp.dot(left, right, precision=lax.Precision.HIGHEST, preferred_element_type=jnp.float32)


def chol_solve_blocked(gram, rhs):
    size = gram.shape[0]
    count = size // BLOCK
    work = (gram + gram.T) * 0.5
    lower = {}
    inverse = []
    eye = jnp.eye(BLOCK, dtype=jnp.float32)
    for k in range(count):
        lo, hi = k * BLOCK, (k + 1) * BLOCK
        diag = jnp.linalg.cholesky(work[lo:hi, lo:hi], symmetrize_input=False)
        inv = lax.linalg.triangular_solve(diag, eye, left_side=True, lower=True, transpose_a=False)
        lower[k, k] = diag
        inverse.append(inv)
        if hi < size:
            panel = exact_dot(work[hi:, lo:hi], inv.T)
            for i in range(k + 1, count):
                lower[i, k] = panel[(i - k - 1) * BLOCK:(i - k) * BLOCK]
            work = work.at[hi:, hi:].add(-exact_dot(panel, panel.T))
    middle = []
    for k in range(count):
        part = rhs[k * BLOCK:(k + 1) * BLOCK]
        if k:
            left = jnp.concatenate([lower[k, j] for j in range(k)], axis=1)
            part = part - exact_dot(left, jnp.concatenate(middle, axis=0))
        middle.append(exact_dot(inverse[k], part))
    solved = [None] * count
    for k in reversed(range(count)):
        part = middle[k]
        if k + 1 < count:
            below = jnp.concatenate([lower[j, k] for j in range(k + 1, count)], axis=0)
            part = part - exact_dot(below.T, jnp.concatenate(solved[k + 1:], axis=0))
        solved[k] = exact_dot(inverse[k].T, part)
    return jnp.concatenate(solved, axis=0)


def split_parts(values):
    upper = values.astype(jnp.bfloat16)
    lower = (values - upper.astype(jnp.float32)).astype(jnp.bfloat16)
    return (upper, lower)


def left_product(feats, other):
    return lax.dot_general(
        feats, other, (((0,), (0,)), ((), ())), preferred_element_type=jnp.float32
    )


def shards(images, labels, predictions, filters, biases):
    share = images.shape[0]
    total_images = share * lax.axis_size("feat") * lax.axis_size("dp")
    piece = lax.all_gather(images, "feat", axis=0, tiled=True)
    feats = conv_pool_fused(piece, filters, biases)
    width = feats.shape[1]
    residual = (
        labels[:, None] == jnp.arange(predictions.shape[1], dtype=jnp.int32)[None, :]
    ).astype(jnp.float32) - predictions
    res_upper, res_lower = split_parts(residual)
    gram = left_product(feats, feats)
    doubled = jnp.concatenate([feats, feats], axis=0)
    cross = left_product(doubled, jnp.concatenate([res_upper, res_lower], axis=0))
    gram, cross = lax.psum((gram, cross), "dp")
    gram = gram / total_images + 0.5 * jnp.eye(width, dtype=jnp.float32)
    cross = cross / total_images
    solved = chol_solve_blocked(gram, cross)
    sol_upper, sol_lower = split_parts(solved)
    fitted = lax.psum_scatter(
        (
            jnp.dot(
                jnp.concatenate([feats, feats], axis=1),
                jnp.concatenate([sol_upper, sol_lower], axis=0),
                preferred_element_type=jnp.float32,
            )
        ).astype(jnp.bfloat16),
        "feat",
        scatter_dimension=0,
        tiled=True,
    ).astype(jnp.float32)
    mine = lax.dynamic_slice_in_dim(residual, lax.axis_index("feat") * share, share, 0)
    return (solved, mine - fitted)


def solution(mesh):
    placed = (P(("dp", "feat"), None), P("dp"), P("dp", None), P(None, "feat"), P("feat"))
    return jax.shard_map(
        shards,
        mesh=mesh,
        in_specs=placed,
        out_specs=(P("feat", None), P(("dp", "feat"), None)),
        check_vma=False,
    )
```

```python
import functools
import math

import jax
import jax.numpy as jnp
from jax import lax
from jax.experimental import pallas as pl
from jax.experimental.pallas import tpu as pltpu
from jax.sharding import PartitionSpec as P

SIDE = 32
CHAN = 3
KSIZE = 5


OUT = SIDE - KSIZE + 1
CHUNK = 7
SPAN = (CHUNK + KSIZE - 1) * CHAN
PITCH = 48
DEPTH = KSIZE * PITCH
TILE = 512


def band_weights(filters, offsets):
    filt_count = filters.shape[1]
    taps = filters.reshape(KSIZE, KSIZE * CHAN, filt_count)
    hi = lax.reduce_precision(offsets, exponent_bits=8, mantissa_bits=7)
    mid = lax.reduce_precision(offsets - hi, exponent_bits=8, mantissa_bits=7)
    lo = offsets - hi - mid
    bias_rows = jnp.stack([hi, mid, lo]).astype(filters.dtype)
    gap = PITCH - SPAN - 3
    blocks = []
    for col in range(CHUNK):
        lead = jnp.zeros((col * CHAN, filt_count), filters.dtype)
        fill = jnp.zeros((SPAN - col * CHAN - KSIZE * CHAN, filt_count), filters.dtype)
        rest = jnp.zeros((PITCH - SPAN, filt_count), filters.dtype)
        first = [lead, taps[0], fill, bias_rows, jnp.zeros((gap, filt_count), filters.dtype)]
        later = [part for ky in range(1, KSIZE) for part in (lead, taps[ky], fill, rest)]
        blocks.append(jnp.concatenate(first + later, axis=0))
    return jnp.transpose(jnp.stack(blocks, axis=0), (0, 2, 1)).reshape(CHUNK * filt_count, DEPTH)


def image_strips(imgs):
    count = imgs.shape[0]
    pics = imgs.reshape(count, SIDE, SIDE * CHAN)
    ones = jnp.ones((count, SIDE, 3), imgs.dtype)
    zeros = jnp.zeros((count, SIDE, PITCH - SPAN - 3), imgs.dtype)
    strips = [
        jnp.concatenate([pics[:, :, CHUNK * CHAN * j: CHUNK * CHAN * j + SPAN], ones, zeros], axis=2)
        for j in range(OUT // CHUNK)
    ]
    stacked = jnp.stack(strips, axis=0)
    return jnp.transpose(stacked, (0, 2, 3, 1)).reshape(OUT // CHUNK, SIDE * PITCH, count)


def pool_kernel(strip_ref, band_ref, out_ref, acc_ref):
    filt_count = out_ref.shape[1]
    half = OUT // 2
    acc_ref[...] = jnp.zeros_like(acc_ref)
    band = band_ref[...]

    def row_step(r, carry, top):
        start = pl.multiple_of(r * PITCH, 16)
        for j in range(OUT // CHUNK):
            patch = strip_ref[j, pl.ds(start, DEPTH), :]
            resp = jnp.dot(band, patch, preferred_element_type=jnp.float32)
            resp = jnp.maximum(resp, 0.0)
            part = resp[0:filt_count]
            for col in range(1, CHUNK):
                part = part + resp[col * filt_count:(col + 1) * filt_count]
            quad = top * 2 + (1 if j >= (OUT // CHUNK) // 2 else 0)
            acc_ref[quad] += part
        return carry

    lax.fori_loop(0, half, functools.partial(row_step, top=0), 0, unroll=2)
    lax.fori_loop(half, OUT, functools.partial(row_step, top=1), 0, unroll=2)
    out_ref[...] = (acc_ref[...] * (1.0 / float(half * half))).astype(out_ref.dtype)


def conv_pool_fused(imgs, filters, offsets):
    count = imgs.shape[0]
    filt_count = filters.shape[1]
    strips = image_strips(imgs)
    band = band_weights(filters, offsets)
    pooled = pl.pallas_call(
        pool_kernel,
        grid=(count // TILE,),
        in_specs=[
            pl.BlockSpec((OUT // CHUNK, SIDE * PITCH, TILE), lambda i: (0, 0, i)),
            pl.BlockSpec((CHUNK * filt_count, DEPTH), lambda i: (0, 0)),
        ],
        out_specs=pl.BlockSpec((4, filt_count, TILE), lambda i: (0, 0, i)),
        out_shape=jax.ShapeDtypeStruct((4, filt_count, count), jnp.bfloat16),
        scratch_shapes=[pltpu.VMEM((4, filt_count, TILE), jnp.float32)],
    )(strips, band)
    return jnp.transpose(pooled, (2, 1, 0)).reshape(count, 4 * filt_count)


BLOCK = 128


def exact_dot(left, right):
    return jnp.dot(left, right, precision=lax.Precision.HIGHEST, preferred_element_type=jnp.float32)


def chol_solve_blocked(gram, rhs):
    size = gram.shape[0]
    count = size // BLOCK
    work = (gram + gram.T) * 0.5
    lower = {}
    inverse = []
    eye = jnp.eye(BLOCK, dtype=jnp.float32)
    for k in range(count):
        lo, hi = k * BLOCK, (k + 1) * BLOCK
        diag = jnp.linalg.cholesky(work[lo:hi, lo:hi], symmetrize_input=False)
        inv = lax.linalg.triangular_solve(diag, eye, left_side=True, lower=True, transpose_a=False)
        lower[k, k] = diag
        inverse.append(inv)
        if hi < size:
            panel = exact_dot(work[hi:, lo:hi], inv.T)
            for i in range(k + 1, count):
                lower[i, k] = panel[(i - k - 1) * BLOCK:(i - k) * BLOCK]
            work = work.at[hi:, hi:].add(-exact_dot(panel, panel.T))
    middle = []
    for k in range(count):
        part = rhs[k * BLOCK:(k + 1) * BLOCK]
        if k:
            left = jnp.concatenate([lower[k, j] for j in range(k)], axis=1)
            part = part - exact_dot(left, jnp.concatenate(middle, axis=0))
        middle.append(exact_dot(inverse[k], part))
    solved = [None] * count
    for k in reversed(range(count)):
        part = middle[k]
        if k + 1 < count:
            below = jnp.concatenate([lower[j, k] for j in range(k + 1, count)], axis=0)
            part = part - exact_dot(below.T, jnp.concatenate(solved[k + 1:], axis=0))
        solved[k] = exact_dot(inverse[k].T, part)
    return jnp.concatenate(solved, axis=0)


def split_parts(values):
    upper = values.astype(jnp.bfloat16)
    lower = (values - upper.astype(jnp.float32)).astype(jnp.bfloat16)
    return (upper, lower)


def left_product(feats, other):
    return lax.dot_general(
        feats, other, (((0,), (0,)), ((), ())), preferred_element_type=jnp.float32
    )


def shards(images, labels, predictions, filters, biases):
    share = images.shape[0]
    total_images = share * lax.axis_size("feat") * lax.axis_size("dp")
    piece = lax.all_gather(images, "feat", axis=0, tiled=True)
    feats = conv_pool_fused(piece, filters, biases)
    width = feats.shape[1]
    residual = (
        labels[:, None] == jnp.arange(predictions.shape[1], dtype=jnp.int32)[None, :]
    ).astype(jnp.float32) - predictions
    res_upper, res_lower = split_parts(residual)
    gram = left_product(feats, feats)
    doubled = jnp.concatenate([feats, feats], axis=0)
    cross = left_product(doubled, jnp.concatenate([res_upper, res_lower], axis=0))
    gram, cross = lax.psum((gram, cross), "dp")
    gram = gram / total_images + 0.5 * jnp.eye(width, dtype=jnp.float32)
    cross = cross / total_images
    solved = chol_solve_blocked(gram, cross)
    sol_upper, sol_lower = split_parts(solved)
    fitted = lax.psum_scatter(
        (
            jnp.dot(
                jnp.concatenate([feats, feats], axis=1),
                jnp.concatenate([sol_upper, sol_lower], axis=0),
                preferred_element_type=jnp.float32,
            )
        ).astype(jnp.bfloat16),
        "feat",
        scatter_dimension=0,
        tiled=True,
    ).astype(jnp.float32)
    mine = lax.dynamic_slice_in_dim(residual, lax.axis_index("feat") * share, share, 0)
    return (solved, mine - fitted)


def solution(mesh):
    placed = (P(("dp", "feat"), None), P("dp"), P("dp", None), P(None, "feat"), P("feat"))
    return jax.shard_map(
        shards,
        mesh=mesh,
        in_specs=placed,
        out_specs=(P("feat", None), P(("dp", "feat"), None)),
        check_vma=False,
    )
```

```python
import functools
import math

import jax
import jax.numpy as jnp
from jax import lax
from jax.experimental import pallas as pl
from jax.experimental.pallas import tpu as pltpu
from jax.sharding import PartitionSpec as P

SIDE = 32
CHAN = 3
KSIZE = 5


OUT = SIDE - KSIZE + 1
CHUNK = 7
SPAN = (CHUNK + KSIZE - 1) * CHAN
PITCH = 48
DEPTH = KSIZE * PITCH
TILE = 512


def band_weights(filters, offsets):
    filt_count = filters.shape[1]
    taps = filters.reshape(KSIZE, KSIZE * CHAN, filt_count)
    hi = lax.reduce_precision(offsets, exponent_bits=8, mantissa_bits=7)
    mid = lax.reduce_precision(offsets - hi, exponent_bits=8, mantissa_bits=7)
    lo = offsets - hi - mid
    bias_rows = jnp.stack([hi, mid, lo]).astype(filters.dtype)
    gap = PITCH - SPAN - 3
    blocks = []
    for col in range(CHUNK):
        lead = jnp.zeros((col * CHAN, filt_count), filters.dtype)
        fill = jnp.zeros((SPAN - col * CHAN - KSIZE * CHAN, filt_count), filters.dtype)
        rest = jnp.zeros((PITCH - SPAN, filt_count), filters.dtype)
        first = [lead, taps[0], fill, bias_rows, jnp.zeros((gap, filt_count), filters.dtype)]
        later = [part for ky in range(1, KSIZE) for part in (lead, taps[ky], fill, rest)]
        blocks.append(jnp.concatenate(first + later, axis=0))
    return jnp.transpose(jnp.stack(blocks, axis=0), (0, 2, 1)).reshape(CHUNK * filt_count, DEPTH)


def image_strips(imgs):
    count = imgs.shape[0]
    pics = imgs.reshape(count, SIDE, SIDE * CHAN)
    ones = jnp.ones((count, SIDE, 3), imgs.dtype)
    zeros = jnp.zeros((count, SIDE, PITCH - SPAN - 3), imgs.dtype)
    strips = [
        jnp.concatenate([pics[:, :, CHUNK * CHAN * j: CHUNK * CHAN * j + SPAN], ones, zeros], axis=2)
        for j in range(OUT // CHUNK)
    ]
    stacked = jnp.stack(strips, axis=0)
    return jnp.transpose(stacked, (0, 2, 3, 1)).reshape(OUT // CHUNK, SIDE * PITCH, count)


def pool_kernel(strip_ref, band_ref, out_ref, acc_ref):
    filt_count = out_ref.shape[1]
    half = OUT // 2
    acc_ref[...] = jnp.zeros_like(acc_ref)
    band = band_ref[...]

    def row_step(r, carry, top):
        start = pl.multiple_of(r * PITCH, 16)
        for j in range(OUT // CHUNK):
            patch = strip_ref[j, pl.ds(start, DEPTH), :]
            resp = jnp.dot(band, patch, preferred_element_type=jnp.float32)
            resp = jnp.maximum(resp, 0.0)
            part = resp[0:filt_count]
            for col in range(1, CHUNK):
                part = part + resp[col * filt_count:(col + 1) * filt_count]
            quad = top * 2 + (1 if j >= (OUT // CHUNK) // 2 else 0)
            acc_ref[quad] += part
        return carry

    lax.fori_loop(0, half, functools.partial(row_step, top=0), 0)
    lax.fori_loop(half, OUT, functools.partial(row_step, top=1), 0)
    out_ref[...] = (acc_ref[...] * (1.0 / float(half * half))).astype(out_ref.dtype)


def conv_pool_fused(imgs, filters, offsets):
    count = imgs.shape[0]
    filt_count = filters.shape[1]
    strips = image_strips(imgs)
    band = band_weights(filters, offsets)
    pooled = pl.pallas_call(
        pool_kernel,
        grid=(count // TILE,),
        in_specs=[
            pl.BlockSpec((OUT // CHUNK, SIDE * PITCH, TILE), lambda i: (0, 0, i)),
            pl.BlockSpec((CHUNK * filt_count, DEPTH), lambda i: (0, 0)),
        ],
        out_specs=pl.BlockSpec((4, filt_count, TILE), lambda i: (0, 0, i)),
        out_shape=jax.ShapeDtypeStruct((4, filt_count, count), jnp.bfloat16),
        scratch_shapes=[pltpu.VMEM((4, filt_count, TILE), jnp.float32)],
    )(strips, band)
    return jnp.transpose(pooled, (2, 1, 0)).reshape(count, 4 * filt_count)


BLOCK = 128


def exact_dot(left, right):
    return jnp.dot(left, right, precision=lax.Precision.HIGHEST, preferred_element_type=jnp.float32)


def chol_solve_blocked(gram, rhs):
    size = gram.shape[0]
    count = size // BLOCK
    work = (gram + gram.T) * 0.5
    lower = {}
    inverse = []
    eye = jnp.eye(BLOCK, dtype=jnp.float32)
    for k in range(count):
        lo, hi = k * BLOCK, (k + 1) * BLOCK
        diag = jnp.linalg.cholesky(work[lo:hi, lo:hi], symmetrize_input=False)
        inv = lax.linalg.triangular_solve(diag, eye, left_side=True, lower=True, transpose_a=False)
        lower[k, k] = diag
        inverse.append(inv)
        if hi < size:
            panel = exact_dot(work[hi:, lo:hi], inv.T)
            for i in range(k + 1, count):
                lower[i, k] = panel[(i - k - 1) * BLOCK:(i - k) * BLOCK]
            work = work.at[hi:, hi:].add(-exact_dot(panel, panel.T))
    middle = []
    for k in range(count):
        part = rhs[k * BLOCK:(k + 1) * BLOCK]
        if k:
            left = jnp.concatenate([lower[k, j] for j in range(k)], axis=1)
            part = part - exact_dot(left, jnp.concatenate(middle, axis=0))
        middle.append(exact_dot(inverse[k], part))
    solved = [None] * count
    for k in reversed(range(count)):
        part = middle[k]
        if k + 1 < count:
            below = jnp.concatenate([lower[j, k] for j in range(k + 1, count)], axis=0)
            part = part - exact_dot(below.T, jnp.concatenate(solved[k + 1:], axis=0))
        solved[k] = exact_dot(inverse[k].T, part)
    return jnp.concatenate(solved, axis=0)


def split_parts(values):
    upper = values.astype(jnp.bfloat16)
    lower = (values - upper.astype(jnp.float32)).astype(jnp.bfloat16)
    return (upper, lower)


def left_product(feats, other):
    return lax.dot_general(
        feats, other, (((0,), (0,)), ((), ())), preferred_element_type=jnp.float32
    )


def shards(images, labels, predictions, filters, biases):
    share = images.shape[0]
    total_images = share * lax.axis_size("feat") * lax.axis_size("dp")
    piece = lax.all_gather(images, "feat", axis=0, tiled=True)
    feats = conv_pool_fused(piece, filters, biases)
    width = feats.shape[1]
    residual = (
        labels[:, None] == jnp.arange(predictions.shape[1], dtype=jnp.int32)[None, :]
    ).astype(jnp.float32) - predictions
    res_upper, res_lower = split_parts(residual)
    gram = left_product(feats, feats)
    doubled = jnp.concatenate([feats, feats], axis=0)
    exact_scale = total_images & (total_images - 1) == 0
    parts = jnp.concatenate([res_upper, res_lower], axis=0)
    if exact_scale:
        parts = parts * jnp.asarray(1.0 / total_images, parts.dtype)
    cross = left_product(doubled, parts)
    gram, cross = lax.psum((gram, cross), "dp")
    gram = gram / total_images + 0.5 * jnp.eye(width, dtype=jnp.float32)
    if not exact_scale:
        cross = cross / total_images
    solved = chol_solve_blocked(gram, cross)
    sol_upper, sol_lower = split_parts(solved)
    fitted = lax.psum_scatter(
        (
            jnp.dot(
                jnp.concatenate([feats, feats], axis=1),
                jnp.concatenate([sol_upper, sol_lower], axis=0),
                preferred_element_type=jnp.float32,
            )
        ).astype(jnp.bfloat16),
        "feat",
        scatter_dimension=0,
        tiled=True,
    ).astype(jnp.float32)
    mine = lax.dynamic_slice_in_dim(residual, lax.axis_index("feat") * share, share, 0)
    return (solved, mine - fitted)


def solution(mesh):
    placed = (P(("dp", "feat"), None), P("dp"), P("dp", None), P(None, "feat"), P("feat"))
    return jax.shard_map(
        shards,
        mesh=mesh,
        in_specs=placed,
        out_specs=(P("feat", None), P(("dp", "feat"), None)),
        check_vma=False,
    )
```

```python
import functools
import math

import jax
import jax.numpy as jnp
from jax import lax
from jax.experimental import pallas as pl
from jax.experimental.pallas import tpu as pltpu
from jax.sharding import PartitionSpec as P

SIDE = 32
CHAN = 3
KSIZE = 5


OUT = SIDE - KSIZE + 1
CHUNK = 7
SPAN = (CHUNK + KSIZE - 1) * CHAN
PITCH = 48
DEPTH = KSIZE * PITCH
TILE = 512


def band_weights(filters, offsets):
    filt_count = filters.shape[1]
    taps = filters.reshape(KSIZE, KSIZE * CHAN, filt_count)
    hi = lax.reduce_precision(offsets, exponent_bits=8, mantissa_bits=7)
    mid = lax.reduce_precision(offsets - hi, exponent_bits=8, mantissa_bits=7)
    lo = offsets - hi - mid
    bias_rows = jnp.stack([hi, mid, lo]).astype(filters.dtype)
    gap = PITCH - SPAN - 3
    blocks = []
    for col in range(CHUNK):
        lead = jnp.zeros((col * CHAN, filt_count), filters.dtype)
        fill = jnp.zeros((SPAN - col * CHAN - KSIZE * CHAN, filt_count), filters.dtype)
        rest = jnp.zeros((PITCH - SPAN, filt_count), filters.dtype)
        first = [lead, taps[0], fill, bias_rows, jnp.zeros((gap, filt_count), filters.dtype)]
        later = [part for ky in range(1, KSIZE) for part in (lead, taps[ky], fill, rest)]
        blocks.append(jnp.concatenate(first + later, axis=0))
    return jnp.transpose(jnp.stack(blocks, axis=0), (0, 2, 1)).reshape(CHUNK * filt_count, DEPTH)


def image_strips(imgs):
    count = imgs.shape[0]
    pics = imgs.reshape(count, SIDE, SIDE * CHAN)
    ones = jnp.ones((count, SIDE, 3), imgs.dtype)
    zeros = jnp.zeros((count, SIDE, PITCH - SPAN - 3), imgs.dtype)
    strips = [
        jnp.concatenate([pics[:, :, CHUNK * CHAN * j: CHUNK * CHAN * j + SPAN], ones, zeros], axis=2)
        for j in range(OUT // CHUNK)
    ]
    stacked = jnp.stack(strips, axis=0)
    return jnp.transpose(stacked, (0, 2, 3, 1)).reshape(OUT // CHUNK, SIDE * PITCH, count)


def pool_kernel(strip_ref, band_ref, out_ref, acc_ref):
    filt_count = out_ref.shape[1]
    half = OUT // 2
    acc_ref[...] = jnp.zeros_like(acc_ref)
    band = band_ref[...]

    def row_step(r, carry, top):
        start = pl.multiple_of(r * PITCH, 16)
        for j in range(OUT // CHUNK):
            patch = strip_ref[j, pl.ds(start, DEPTH), :]
            resp = jnp.dot(band, patch, preferred_element_type=jnp.float32)
            resp = jnp.maximum(resp, 0.0)
            part = resp[0:filt_count]
            for col in range(1, CHUNK):
                part = part + resp[col * filt_count:(col + 1) * filt_count]
            quad = top * 2 + (1 if j >= (OUT // CHUNK) // 2 else 0)
            acc_ref[quad] += part
        return carry

    lax.fori_loop(0, half, functools.partial(row_step, top=0), 0)
    lax.fori_loop(half, OUT, functools.partial(row_step, top=1), 0)
    out_ref[...] = (acc_ref[...] * (1.0 / float(half * half))).astype(out_ref.dtype)


def conv_pool_fused(imgs, filters, offsets):
    count = imgs.shape[0]
    filt_count = filters.shape[1]
    strips = image_strips(imgs)
    band = band_weights(filters, offsets)
    pooled = pl.pallas_call(
        pool_kernel,
        grid=(count // TILE,),
        in_specs=[
            pl.BlockSpec((OUT // CHUNK, SIDE * PITCH, TILE), lambda i: (0, 0, i)),
            pl.BlockSpec((CHUNK * filt_count, DEPTH), lambda i: (0, 0)),
        ],
        out_specs=pl.BlockSpec((4, filt_count, TILE), lambda i: (0, 0, i)),
        out_shape=jax.ShapeDtypeStruct((4, filt_count, count), jnp.bfloat16),
        scratch_shapes=[pltpu.VMEM((4, filt_count, TILE), jnp.float32)],
    )(strips, band)
    return jnp.transpose(pooled, (2, 1, 0)).reshape(count, 4 * filt_count)


BLOCK = 128


def exact_dot(left, right):
    return jnp.dot(left, right, precision=lax.Precision.HIGHEST, preferred_element_type=jnp.float32)


def chol_solve_blocked(gram, rhs):
    size = gram.shape[0]
    count = size // BLOCK
    work = (gram + gram.T) * 0.5
    lower = {}
    inverse = []
    eye = jnp.eye(BLOCK, dtype=jnp.float32)
    for k in range(count):
        lo, hi = k * BLOCK, (k + 1) * BLOCK
        diag = jnp.linalg.cholesky(work[lo:hi, lo:hi], symmetrize_input=False)
        inv = lax.linalg.triangular_solve(diag, eye, left_side=True, lower=True, transpose_a=False)
        lower[k, k] = diag
        inverse.append(inv)
        if hi < size:
            panel = exact_dot(work[hi:, lo:hi], inv.T)
            for i in range(k + 1, count):
                lower[i, k] = panel[(i - k - 1) * BLOCK:(i - k) * BLOCK]
            work = work.at[hi:, hi:].add(-exact_dot(panel, panel.T))
    middle = []
    for k in range(count):
        part = rhs[k * BLOCK:(k + 1) * BLOCK]
        if k:
            left = jnp.concatenate([lower[k, j] for j in range(k)], axis=1)
            part = part - exact_dot(left, jnp.concatenate(middle, axis=0))
        middle.append(exact_dot(inverse[k], part))
    solved = [None] * count
    for k in reversed(range(count)):
        part = middle[k]
        if k + 1 < count:
            below = jnp.concatenate([lower[j, k] for j in range(k + 1, count)], axis=0)
            part = part - exact_dot(below.T, jnp.concatenate(solved[k + 1:], axis=0))
        solved[k] = exact_dot(inverse[k].T, part)
    return jnp.concatenate(solved, axis=0)


def split_parts(values):
    upper = values.astype(jnp.bfloat16)
    lower = (values - upper.astype(jnp.float32)).astype(jnp.bfloat16)
    return (upper, lower)


def left_product(feats, other):
    return lax.dot_general(
        feats, other, (((0,), (0,)), ((), ())), preferred_element_type=jnp.float32
    )


def shards(images, labels, predictions, filters, biases):
    share = images.shape[0]
    total_images = share * lax.axis_size("feat") * lax.axis_size("dp")
    piece = lax.all_gather(images, "feat", axis=0, tiled=True)
    feats = conv_pool_fused(piece, filters, biases)
    width = feats.shape[1]
    residual = (
        labels[:, None] == jnp.arange(predictions.shape[1], dtype=jnp.int32)[None, :]
    ).astype(jnp.float32) - predictions
    res_upper, res_lower = split_parts(residual)
    doubled = jnp.concatenate([feats, feats], axis=0)
    spare = jnp.zeros_like(feats)
    right = jnp.concatenate(
        [jnp.concatenate([feats, spare], axis=0), jnp.concatenate([res_upper, res_lower], axis=0)], axis=1
    )
    both = lax.psum(left_product(doubled, right), "dp")
    gram, cross = both[:, :width], both[:, width:]
    gram = gram / total_images + 0.5 * jnp.eye(width, dtype=jnp.float32)
    cross = cross / total_images
    solved = chol_solve_blocked(gram, cross)
    sol_upper, sol_lower = split_parts(solved)
    fitted = lax.psum_scatter(
        (
            jnp.dot(
                jnp.concatenate([feats, feats], axis=1),
                jnp.concatenate([sol_upper, sol_lower], axis=0),
                preferred_element_type=jnp.float32,
            )
        ).astype(jnp.bfloat16),
        "feat",
        scatter_dimension=0,
        tiled=True,
    ).astype(jnp.float32)
    mine = lax.dynamic_slice_in_dim(residual, lax.axis_index("feat") * share, share, 0)
    return (solved, mine - fitted)


def solution(mesh):
    placed = (P(("dp", "feat"), None), P("dp"), P("dp", None), P(None, "feat"), P("feat"))
    return jax.shard_map(
        shards,
        mesh=mesh,
        in_specs=placed,
        out_specs=(P("feat", None), P(("dp", "feat"), None)),
        check_vma=False,
    )
```

```python
import functools
import math

import jax
import jax.numpy as jnp
from jax import lax
from jax.experimental import pallas as pl
from jax.experimental.pallas import tpu as pltpu
from jax.sharding import PartitionSpec as P

SIDE = 32
CHAN = 3
KSIZE = 5


OUT = SIDE - KSIZE + 1
CHUNK = 7
SPAN = (CHUNK + KSIZE - 1) * CHAN
PITCH = 48
DEPTH = KSIZE * PITCH
TILE = 512


def band_weights(filters, offsets):
    filt_count = filters.shape[1]
    taps = filters.reshape(KSIZE, KSIZE * CHAN, filt_count)
    hi = lax.reduce_precision(offsets, exponent_bits=8, mantissa_bits=7)
    mid = lax.reduce_precision(offsets - hi, exponent_bits=8, mantissa_bits=7)
    lo = offsets - hi - mid
    bias_rows = jnp.stack([hi, mid, lo]).astype(filters.dtype)
    gap = PITCH - SPAN - 3
    blocks = []
    for col in range(CHUNK):
        lead = jnp.zeros((col * CHAN, filt_count), filters.dtype)
        fill = jnp.zeros((SPAN - col * CHAN - KSIZE * CHAN, filt_count), filters.dtype)
        rest = jnp.zeros((PITCH - SPAN, filt_count), filters.dtype)
        first = [lead, taps[0], fill, bias_rows, jnp.zeros((gap, filt_count), filters.dtype)]
        later = [part for ky in range(1, KSIZE) for part in (lead, taps[ky], fill, rest)]
        blocks.append(jnp.concatenate(first + later, axis=0))
    return jnp.transpose(jnp.stack(blocks, axis=0), (0, 2, 1)).reshape(CHUNK * filt_count, DEPTH)


def image_strips(imgs):
    count = imgs.shape[0]
    pics = imgs.reshape(count, SIDE, SIDE * CHAN)
    ones = jnp.ones((count, SIDE, 3), imgs.dtype)
    zeros = jnp.zeros((count, SIDE, PITCH - SPAN - 3), imgs.dtype)
    strips = [
        jnp.concatenate([pics[:, :, CHUNK * CHAN * j: CHUNK * CHAN * j + SPAN], ones, zeros], axis=2)
        for j in range(OUT // CHUNK)
    ]
    stacked = jnp.stack(strips, axis=0)
    return jnp.transpose(stacked, (0, 2, 3, 1)).reshape(OUT // CHUNK, SIDE * PITCH, count)


def pool_kernel(strip_ref, band_ref, out_ref, acc_ref):
    filt_count = out_ref.shape[1]
    half = OUT // 2
    acc_ref[...] = jnp.zeros_like(acc_ref)
    band = band_ref[...]

    def row_step(r, carry, top):
        start = pl.multiple_of(r * PITCH, 16)
        sides = [None, None]
        for j in range(OUT // CHUNK):
            patch = strip_ref[j, pl.ds(start, DEPTH), :]
            resp = jnp.dot(band, patch, preferred_element_type=jnp.float32)
            resp = jnp.maximum(resp, 0.0)
            part = resp[0:filt_count]
            for col in range(1, CHUNK):
                part = part + resp[col * filt_count:(col + 1) * filt_count]
            side = 1 if j >= (OUT // CHUNK) // 2 else 0
            sides[side] = part if sides[side] is None else sides[side] + part
        for side in range(2):
            acc_ref[top * 2 + side] += sides[side]
        return carry

    lax.fori_loop(0, half, functools.partial(row_step, top=0), 0)
    lax.fori_loop(half, OUT, functools.partial(row_step, top=1), 0)
    out_ref[...] = (acc_ref[...] * (1.0 / float(half * half))).astype(out_ref.dtype)


def conv_pool_fused(imgs, filters, offsets):
    count = imgs.shape[0]
    filt_count = filters.shape[1]
    strips = image_strips(imgs)
    band = band_weights(filters, offsets)
    pooled = pl.pallas_call(
        pool_kernel,
        grid=(count // TILE,),
        in_specs=[
            pl.BlockSpec((OUT // CHUNK, SIDE * PITCH, TILE), lambda i: (0, 0, i)),
            pl.BlockSpec((CHUNK * filt_count, DEPTH), lambda i: (0, 0)),
        ],
        out_specs=pl.BlockSpec((4, filt_count, TILE), lambda i: (0, 0, i)),
        out_shape=jax.ShapeDtypeStruct((4, filt_count, count), jnp.bfloat16),
        scratch_shapes=[pltpu.VMEM((4, filt_count, TILE), jnp.float32)],
    )(strips, band)
    return jnp.transpose(pooled, (2, 1, 0)).reshape(count, 4 * filt_count)


BLOCK = 128


def exact_dot(left, right):
    return jnp.dot(left, right, precision=lax.Precision.HIGHEST, preferred_element_type=jnp.float32)


def chol_solve_blocked(gram, rhs):
    size = gram.shape[0]
    count = size // BLOCK
    work = (gram + gram.T) * 0.5
    lower = {}
    inverse = []
    eye = jnp.eye(BLOCK, dtype=jnp.float32)
    for k in range(count):
        lo, hi = k * BLOCK, (k + 1) * BLOCK
        diag = jnp.linalg.cholesky(work[lo:hi, lo:hi], symmetrize_input=False)
        inv = lax.linalg.triangular_solve(diag, eye, left_side=True, lower=True, transpose_a=False)
        lower[k, k] = diag
        inverse.append(inv)
        if hi < size:
            panel = exact_dot(work[hi:, lo:hi], inv.T)
            for i in range(k + 1, count):
                lower[i, k] = panel[(i - k - 1) * BLOCK:(i - k) * BLOCK]
            work = work.at[hi:, hi:].add(-exact_dot(panel, panel.T))
    middle = []
    for k in range(count):
        part = rhs[k * BLOCK:(k + 1) * BLOCK]
        if k:
            left = jnp.concatenate([lower[k, j] for j in range(k)], axis=1)
            part = part - exact_dot(left, jnp.concatenate(middle, axis=0))
        middle.append(exact_dot(inverse[k], part))
    solved = [None] * count
    for k in reversed(range(count)):
        part = middle[k]
        if k + 1 < count:
            below = jnp.concatenate([lower[j, k] for j in range(k + 1, count)], axis=0)
            part = part - exact_dot(below.T, jnp.concatenate(solved[k + 1:], axis=0))
        solved[k] = exact_dot(inverse[k].T, part)
    return jnp.concatenate(solved, axis=0)


def split_parts(values):
    upper = values.astype(jnp.bfloat16)
    lower = (values - upper.astype(jnp.float32)).astype(jnp.bfloat16)
    return (upper, lower)


def left_product(feats, other):
    return lax.dot_general(
        feats, other, (((0,), (0,)), ((), ())), preferred_element_type=jnp.float32
    )


def shards(images, labels, predictions, filters, biases):
    share = images.shape[0]
    total_images = share * lax.axis_size("feat") * lax.axis_size("dp")
    piece = lax.all_gather(images, "feat", axis=0, tiled=True)
    feats = conv_pool_fused(piece, filters, biases)
    width = feats.shape[1]
    residual = (
        labels[:, None] == jnp.arange(predictions.shape[1], dtype=jnp.int32)[None, :]
    ).astype(jnp.float32) - predictions
    res_upper, res_lower = split_parts(residual)
    gram = left_product(feats, feats)
    doubled = jnp.concatenate([feats, feats], axis=0)
    cross = left_product(doubled, jnp.concatenate([res_upper, res_lower], axis=0))
    gram, cross = lax.psum((gram, cross), "dp")
    gram = gram / total_images + 0.5 * jnp.eye(width, dtype=jnp.float32)
    cross = cross / total_images
    solved = chol_solve_blocked(gram, cross)
    sol_upper, sol_lower = split_parts(solved)
    fitted = lax.psum_scatter(
        (
            jnp.dot(
                jnp.concatenate([feats, feats], axis=1),
                jnp.concatenate([sol_upper, sol_lower], axis=0),
                preferred_element_type=jnp.float32,
            )
        ).astype(jnp.bfloat16),
        "feat",
        scatter_dimension=0,
        tiled=True,
    ).astype(jnp.float32)
    mine = lax.dynamic_slice_in_dim(residual, lax.axis_index("feat") * share, share, 0)
    return (solved, mine - fitted)


def solution(mesh):
    placed = (P(("dp", "feat"), None), P("dp"), P("dp", None), P(None, "feat"), P("feat"))
    return jax.shard_map(
        shards,
        mesh=mesh,
        in_specs=placed,
        out_specs=(P("feat", None), P(("dp", "feat"), None)),
        check_vma=False,
    )
```

```python
import functools
import math

import jax
import jax.numpy as jnp
from jax import lax
from jax.experimental import pallas as pl
from jax.experimental.pallas import tpu as pltpu
from jax.sharding import PartitionSpec as P

SIDE = 32
CHAN = 3
KSIZE = 5


OUT = SIDE - KSIZE + 1
CHUNK = 7
SPAN = (CHUNK + KSIZE - 1) * CHAN
PITCH = 48
DEPTH = KSIZE * PITCH
TILE = 512


def band_weights(filters, offsets):
    filt_count = filters.shape[1]
    taps = filters.reshape(KSIZE, KSIZE * CHAN, filt_count)
    hi = lax.reduce_precision(offsets, exponent_bits=8, mantissa_bits=7)
    mid = lax.reduce_precision(offsets - hi, exponent_bits=8, mantissa_bits=7)
    lo = offsets - hi - mid
    bias_rows = jnp.stack([hi, mid, lo]).astype(filters.dtype)
    gap = PITCH - SPAN - 3
    blocks = []
    for col in range(CHUNK):
        lead = jnp.zeros((col * CHAN, filt_count), filters.dtype)
        fill = jnp.zeros((SPAN - col * CHAN - KSIZE * CHAN, filt_count), filters.dtype)
        rest = jnp.zeros((PITCH - SPAN, filt_count), filters.dtype)
        first = [lead, taps[0], fill, bias_rows, jnp.zeros((gap, filt_count), filters.dtype)]
        later = [part for ky in range(1, KSIZE) for part in (lead, taps[ky], fill, rest)]
        blocks.append(jnp.concatenate(first + later, axis=0))
    return jnp.transpose(jnp.stack(blocks, axis=0), (0, 2, 1)).reshape(CHUNK * filt_count, DEPTH)


def image_strips(imgs):
    count = imgs.shape[0]
    pics = imgs.reshape(count, SIDE, SIDE * CHAN)
    ones = jnp.ones((count, SIDE, 3), imgs.dtype)
    zeros = jnp.zeros((count, SIDE, PITCH - SPAN - 3), imgs.dtype)
    strips = [
        jnp.concatenate([pics[:, :, CHUNK * CHAN * j: CHUNK * CHAN * j + SPAN], ones, zeros], axis=2)
        for j in range(OUT // CHUNK)
    ]
    stacked = jnp.stack(strips, axis=0)
    return jnp.transpose(stacked, (0, 2, 3, 1)).reshape(OUT // CHUNK, SIDE * PITCH, count)


def pool_kernel(strip_ref, band_ref, out_ref, acc_ref):
    filt_count = out_ref.shape[1]
    half = OUT // 2
    acc_ref[...] = jnp.zeros_like(acc_ref)
    band = band_ref[...]

    def row_step(r, carry, top):
        start = pl.multiple_of(r * PITCH, 16)
        for j in range(OUT // CHUNK):
            patch = strip_ref[j, pl.ds(start, DEPTH), :]
            resp = jnp.dot(band, patch, preferred_element_type=jnp.float32)
            resp = jnp.maximum(resp, 0.0)
            part = resp[0:filt_count]
            for col in range(1, CHUNK):
                part = part + resp[col * filt_count:(col + 1) * filt_count]
            quad = top * 2 + (1 if j >= (OUT // CHUNK) // 2 else 0)
            acc_ref[quad] += part
        return carry

    lax.fori_loop(0, half, functools.partial(row_step, top=0), 0)
    lax.fori_loop(half, OUT, functools.partial(row_step, top=1), 0)
    out_ref[...] = (acc_ref[...] * (1.0 / float(half * half))).astype(out_ref.dtype)


def conv_pool_fused(imgs, filters, offsets):
    count = imgs.shape[0]
    filt_count = filters.shape[1]
    strips = image_strips(imgs)
    band = band_weights(filters, offsets)
    pooled = pl.pallas_call(
        pool_kernel,
        grid=(count // TILE,),
        in_specs=[
            pl.BlockSpec((OUT // CHUNK, SIDE * PITCH, TILE), lambda i: (0, 0, i)),
            pl.BlockSpec((CHUNK * filt_count, DEPTH), lambda i: (0, 0)),
        ],
        out_specs=pl.BlockSpec((4, filt_count, TILE), lambda i: (0, 0, i)),
        out_shape=jax.ShapeDtypeStruct((4, filt_count, count), jnp.bfloat16),
        scratch_shapes=[pltpu.VMEM((4, filt_count, TILE), jnp.float32)],
    )(strips, band)
    return jnp.transpose(pooled, (2, 1, 0)).reshape(count, 4 * filt_count)


BLOCK = 128


def exact_dot(left, right):
    return jnp.dot(left, right, precision=lax.Precision.HIGHEST, preferred_element_type=jnp.float32)


def chol_solve_blocked(gram, rhs):
    size = gram.shape[0]
    count = size // BLOCK
    work = gram
    lower = {}
    inverse = []
    eye = jnp.eye(BLOCK, dtype=jnp.float32)
    for k in range(count):
        lo, hi = k * BLOCK, (k + 1) * BLOCK
        diag = jnp.linalg.cholesky(work[lo:hi, lo:hi], symmetrize_input=False)
        inv = lax.linalg.triangular_solve(diag, eye, left_side=True, lower=True, transpose_a=False)
        lower[k, k] = diag
        inverse.append(inv)
        if hi < size:
            panel = exact_dot(work[hi:, lo:hi], inv.T)
            for i in range(k + 1, count):
                lower[i, k] = panel[(i - k - 1) * BLOCK:(i - k) * BLOCK]
            work = work.at[hi:, hi:].add(-exact_dot(panel, panel.T))
    middle = []
    for k in range(count):
        part = rhs[k * BLOCK:(k + 1) * BLOCK]
        if k:
            left = jnp.concatenate([lower[k, j] for j in range(k)], axis=1)
            part = part - exact_dot(left, jnp.concatenate(middle, axis=0))
        middle.append(exact_dot(inverse[k], part))
    solved = [None] * count
    for k in reversed(range(count)):
        part = middle[k]
        if k + 1 < count:
            below = jnp.concatenate([lower[j, k] for j in range(k + 1, count)], axis=0)
            part = part - exact_dot(below.T, jnp.concatenate(solved[k + 1:], axis=0))
        solved[k] = exact_dot(inverse[k].T, part)
    return jnp.concatenate(solved, axis=0)


def split_parts(values):
    upper = values.astype(jnp.bfloat16)
    lower = (values - upper.astype(jnp.float32)).astype(jnp.bfloat16)
    return (upper, lower)


def left_product(feats, other):
    return lax.dot_general(
        feats, other, (((0,), (0,)), ((), ())), preferred_element_type=jnp.float32
    )


def shards(images, labels, predictions, filters, biases):
    share = images.shape[0]
    total_images = share * lax.axis_size("feat") * lax.axis_size("dp")
    piece = lax.all_gather(images, "feat", axis=0, tiled=True)
    feats = conv_pool_fused(piece, filters, biases)
    width = feats.shape[1]
    residual = (
        labels[:, None] == jnp.arange(predictions.shape[1], dtype=jnp.int32)[None, :]
    ).astype(jnp.float32) - predictions
    res_upper, res_lower = split_parts(residual)
    gram = left_product(feats, feats)
    doubled = jnp.concatenate([feats, feats], axis=0)
    cross = left_product(doubled, jnp.concatenate([res_upper, res_lower], axis=0))
    gram, cross = lax.psum((gram, cross), "dp")
    gram = gram / total_images + 0.5 * jnp.eye(width, dtype=jnp.float32)
    cross = cross / total_images
    solved = chol_solve_blocked(gram, cross)
    sol_upper, sol_lower = split_parts(solved)
    fitted = lax.psum_scatter(
        (
            jnp.dot(
                jnp.concatenate([feats, feats], axis=1),
                jnp.concatenate([sol_upper, sol_lower], axis=0),
                preferred_element_type=jnp.float32,
            )
        ).astype(jnp.bfloat16),
        "feat",
        scatter_dimension=0,
        tiled=True,
    ).astype(jnp.float32)
    mine = lax.dynamic_slice_in_dim(residual, lax.axis_index("feat") * share, share, 0)
    return (solved, mine - fitted)


def solution(mesh):
    placed = (P(("dp", "feat"), None), P("dp"), P("dp", None), P(None, "feat"), P("feat"))
    return jax.shard_map(
        shards,
        mesh=mesh,
        in_specs=placed,
        out_specs=(P("feat", None), P(("dp", "feat"), None)),
        check_vma=False,
    )
```

```python
import functools
import math

import jax
import jax.numpy as jnp
from jax import lax
from jax.experimental import pallas as pl
from jax.experimental.pallas import tpu as pltpu
from jax.sharding import PartitionSpec as P

SIDE = 32
CHAN = 3
KSIZE = 5


OUT = SIDE - KSIZE + 1
CHUNK = 7
SPAN = (CHUNK + KSIZE - 1) * CHAN
PITCH = 48
DEPTH = KSIZE * PITCH
TILE = 512


def band_weights(filters, offsets):
    filt_count = filters.shape[1]
    taps = filters.reshape(KSIZE, KSIZE * CHAN, filt_count)
    hi = lax.reduce_precision(offsets, exponent_bits=8, mantissa_bits=7)
    mid = lax.reduce_precision(offsets - hi, exponent_bits=8, mantissa_bits=7)
    lo = offsets - hi - mid
    bias_rows = jnp.stack([hi, mid, lo]).astype(filters.dtype)
    gap = PITCH - SPAN - 3
    blocks = []
    for col in range(CHUNK):
        lead = jnp.zeros((col * CHAN, filt_count), filters.dtype)
        fill = jnp.zeros((SPAN - col * CHAN - KSIZE * CHAN, filt_count), filters.dtype)
        rest = jnp.zeros((PITCH - SPAN, filt_count), filters.dtype)
        first = [lead, taps[0], fill, bias_rows, jnp.zeros((gap, filt_count), filters.dtype)]
        later = [part for ky in range(1, KSIZE) for part in (lead, taps[ky], fill, rest)]
        blocks.append(jnp.concatenate(first + later, axis=0))
    return jnp.transpose(jnp.stack(blocks, axis=0), (0, 2, 1)).reshape(CHUNK * filt_count, DEPTH)


def image_strips(imgs):
    count = imgs.shape[0]
    pics = imgs.reshape(count, SIDE, SIDE * CHAN)
    ones = jnp.ones((count, SIDE, 3), imgs.dtype)
    zeros = jnp.zeros((count, SIDE, PITCH - SPAN - 3), imgs.dtype)
    strips = [
        jnp.concatenate([pics[:, :, CHUNK * CHAN * j: CHUNK * CHAN * j + SPAN], ones, zeros], axis=2)
        for j in range(OUT // CHUNK)
    ]
    stacked = jnp.stack(strips, axis=0)
    return jnp.transpose(stacked, (0, 2, 3, 1)).reshape(OUT // CHUNK, SIDE * PITCH, count)


def pool_kernel(strip_ref, band_ref, out_ref, acc_ref):
    filt_count = out_ref.shape[1]
    half = OUT // 2
    acc_ref[...] = jnp.zeros_like(acc_ref)
    band = band_ref[...]

    def row_step(r, carry, top):
        start = pl.multiple_of(r * PITCH, 16)
        for j in range(OUT // CHUNK):
            patch = strip_ref[j, pl.ds(start, DEPTH), :]
            resp = jnp.dot(band, patch, preferred_element_type=jnp.float32)
            resp = jnp.maximum(resp, 0.0)
            part = resp[0:filt_count]
            for col in range(1, CHUNK):
                part = part + resp[col * filt_count:(col + 1) * filt_count]
            quad = top * 2 + (1 if j >= (OUT // CHUNK) // 2 else 0)
            acc_ref[quad] += part
        return carry

    lax.fori_loop(0, half, functools.partial(row_step, top=0), 0)
    lax.fori_loop(half, OUT, functools.partial(row_step, top=1), 0)
    out_ref[...] = (acc_ref[...] * (1.0 / float(half * half))).astype(out_ref.dtype)


def conv_pool_fused(imgs, filters, offsets):
    count = imgs.shape[0]
    filt_count = filters.shape[1]
    strips = image_strips(imgs)
    band = band_weights(filters, offsets)
    pooled = pl.pallas_call(
        pool_kernel,
        grid=(count // TILE,),
        in_specs=[
            pl.BlockSpec((OUT // CHUNK, SIDE * PITCH, TILE), lambda i: (0, 0, i)),
            pl.BlockSpec((CHUNK * filt_count, DEPTH), lambda i: (0, 0)),
        ],
        out_specs=pl.BlockSpec((4, filt_count, TILE), lambda i: (0, 0, i)),
        out_shape=jax.ShapeDtypeStruct((4, filt_count, count), jnp.bfloat16),
        scratch_shapes=[pltpu.VMEM((4, filt_count, TILE), jnp.float32)],
    )(strips, band)
    return jnp.transpose(pooled, (2, 1, 0)).reshape(count, 4 * filt_count)


BLOCK = 128


def exact_dot(left, right):
    return jnp.dot(left, right, precision=lax.Precision.HIGHEST, preferred_element_type=jnp.float32)


def chol_solve_blocked(gram, rhs):
    size = gram.shape[0]
    count = size // BLOCK
    work = gram
    lower = {}
    inverse = []
    eye = jnp.eye(BLOCK, dtype=jnp.float32)
    for k in range(count):
        lo, hi = k * BLOCK, (k + 1) * BLOCK
        diag = jnp.linalg.cholesky(work[lo:hi, lo:hi], symmetrize_input=False)
        inv = lax.linalg.triangular_solve(diag, eye, left_side=True, lower=True, transpose_a=False)
        lower[k, k] = diag
        inverse.append(inv)
        if hi < size:
            panel = exact_dot(work[hi:, lo:hi], inv.T)
            for i in range(k + 1, count):
                lower[i, k] = panel[(i - k - 1) * BLOCK:(i - k) * BLOCK]
            work = work.at[hi:, hi:].add(-exact_dot(panel, panel.T))
    middle = []
    for k in range(count):
        part = rhs[k * BLOCK:(k + 1) * BLOCK]
        if k:
            left = jnp.concatenate([lower[k, j] for j in range(k)], axis=1)
            part = part - exact_dot(left, jnp.concatenate(middle, axis=0))
        middle.append(exact_dot(inverse[k], part))
    solved = [None] * count
    for k in reversed(range(count)):
        part = middle[k]
        if k + 1 < count:
            below = jnp.concatenate([lower[j, k] for j in range(k + 1, count)], axis=0)
            part = part - exact_dot(below.T, jnp.concatenate(solved[k + 1:], axis=0))
        solved[k] = exact_dot(inverse[k].T, part)
    return jnp.concatenate(solved, axis=0)


def split_parts(values):
    upper = values.astype(jnp.bfloat16)
    lower = (values - upper.astype(jnp.float32)).astype(jnp.bfloat16)
    return (upper, lower)


def left_product(feats, other):
    return lax.dot_general(
        feats, other, (((0,), (0,)), ((), ())), preferred_element_type=jnp.float32
    )


def shards(images, labels, predictions, filters, biases):
    share = images.shape[0]
    total_images = share * lax.axis_size("feat") * lax.axis_size("dp")
    piece = lax.all_gather(images, "feat", axis=0, tiled=True)
    feats = conv_pool_fused(piece, filters, biases)
    width = feats.shape[1]
    residual = (
        labels[:, None] == jnp.arange(predictions.shape[1], dtype=jnp.int32)[None, :]
    ).astype(jnp.float32) - predictions
    res_upper, res_lower = split_parts(residual)
    exact_gram = total_images & (total_images - 1) == 0
    scaled = feats * jnp.asarray(1.0 / total_images, feats.dtype) if exact_gram else feats
    gram = left_product(scaled, feats)
    doubled = jnp.concatenate([feats, feats], axis=0)
    cross = left_product(doubled, jnp.concatenate([res_upper, res_lower], axis=0))
    gram, cross = lax.psum((gram, cross), "dp")
    if not exact_gram:
        gram = gram / total_images
    gram = gram + 0.5 * jnp.eye(width, dtype=jnp.float32)
    cross = cross / total_images
    solved = chol_solve_blocked(gram, cross)
    sol_upper, sol_lower = split_parts(solved)
    fitted = lax.psum_scatter(
        (
            jnp.dot(
                jnp.concatenate([feats, feats], axis=1),
                jnp.concatenate([sol_upper, sol_lower], axis=0),
                preferred_element_type=jnp.float32,
            )
        ).astype(jnp.bfloat16),
        "feat",
        scatter_dimension=0,
        tiled=True,
    ).astype(jnp.float32)
    mine = lax.dynamic_slice_in_dim(residual, lax.axis_index("feat") * share, share, 0)
    return (solved, mine - fitted)


def solution(mesh):
    placed = (P(("dp", "feat"), None), P("dp"), P("dp", None), P(None, "feat"), P("feat"))
    return jax.shard_map(
        shards,
        mesh=mesh,
        in_specs=placed,
        out_specs=(P("feat", None), P(("dp", "feat"), None)),
        check_vma=False,
    )
```
